32 devices in a mesh: clip: 4 (over z), seg: 8 (over y, x, core).
Axes of the slice: x: 2, y: 2, z: 4, core: 2. Of those that a mesh axis runs over, the one named last changes fastest.
Arguments:
- spectra: bfloat16 [16, 2, 1024, 192], P('clip', None, 'seg'), may hold values from -6 to 6
- target: bfloat16 [16, 98304], P('clip', 'seg'), may hold values from -12 to 12
- lengths: int32 [16], P('clip'), may hold values from 96 to 192, as said below
Outputs:
- loss: float32 [], replicated
- spec_grad: bfloat16 [16, 2, 1024, 192], P('clip', None, 'seg')
The draws below stay inside these ranges and needn't reach their ends.
Inputs may be any that keep to these rules, and one draw needn't show every extreme that they name: `lengths`: some clip has all 192 frames.
All inputs are finite; a program needn't handle non-finite values.
Results may differ from the reference program's by a relative error of at most 0.0092.
Values may be sent and summed in bfloat16 or wider, within the bound.
No kernel may reach another device: no remote copies, remote signals or barrier semaphores. Data moves between devices by JAX's collectives and lax.ppermute only.
A program may use at most 128 MiB of HBM per device.

```python
import math
import jax
import jax.numpy as jnp
from jax import lax

BINS = 1024
NFFT = 2048
HOP = 512
CLIPS = 16
FRAMES = 192
SAMPLES = 98304


def draw_target(key, part):
    gaussian = jax.random.normal(jax.random.fold_in(key, 11), (CLIPS, SAMPLES), jnp.float32)
    position = jnp.arange(SAMPLES).astype(jnp.float32) / SAMPLES
    signal = gaussian * jnp.sqrt(1.0 + 2.0 * position)[None, :]
    return jnp.clip(signal, -12.0, 12.0).astype(jnp.bfloat16)


def draw_lengths(key, part):
    drawn = jax.random.randint(jax.random.fold_in(key, 21), (CLIPS,), FRAMES // 2, FRAMES + 1)
    longest = jax.random.randint(jax.random.fold_in(key, 22), (), 0, CLIPS)
    return jnp.where(jnp.arange(CLIPS) == longest, FRAMES, drawn).astype(jnp.int32)


def block_scale(rng, extent, shards, least, top_value):
    gain = 1.0
    for axis_at, parts in shards:
        draws = jax.random.uniform(jax.random.fold_in(jax.random.fold_in(rng, 6), axis_at), (parts,), jnp.float32, least / len(shards), top_value / len(shards))
        gain = gain * jnp.repeat(jnp.exp(draws), extent[axis_at] // parts).reshape((-1,) + (1,) * (len(extent) - 1 - axis_at))
    return gain


def bell_draw(key, dims, width, reach, cuts=(), kind=jnp.bfloat16):
    values = width * jax.random.normal(key, dims, jnp.float32)
    if cuts:
        values = values * block_scale(key, dims, cuts, -0.22, 0.18)
    return jnp.clip(values, -reach, reach).astype(kind)


def setup_inputs(seed: int = 0) -> dict:
    seeds = jax.random.split(jax.random.key(seed), 4)
    spectra = bell_draw(seeds[0], (CLIPS, 2, BINS, FRAMES), 1.0, 6.0, ((0, 4), (2, 8)))
    target = draw_target(jax.random.fold_in(seeds[3], 71), 0)
    lengths = draw_lengths(jax.random.fold_in(seeds[3], 71), 0)
    return {"spectra": spectra, "target": target, "lengths": lengths}


EPS_MAG = 0.1
EPS_RATIO = 1e-05

def wave_table(bins_index, time_index, points, factor):
    halfway = points // 2
    is_sine = bins_index >= halfway
    harmonic = jnp.where(is_sine, bins_index - halfway, bins_index)
    angles = (harmonic * time_index % points).astype(jnp.float32) * (2.0 * math.pi / points)
    window = 0.5 - 0.5 * jnp.cos(time_index.astype(jnp.float32) * (2.0 * math.pi / points))
    entry_value = jnp.where(is_sine, -jnp.sin(angles), jnp.cos(angles))
    return (entry_value * window * factor).astype(jnp.bfloat16)

def frame_rows(signal, points):
    stride = points // 4
    frame_count = signal.shape[0] // stride
    padded = jnp.concatenate([signal, jnp.zeros((3 * stride,), signal.dtype)]).reshape(frame_count + 3, stride)
    return jnp.concatenate([padded[quarter:quarter + frame_count] for quarter in range(4)], axis=1)

def intersection_rows(framed, points):
    stride = points // 4
    frame_count = framed.shape[0]
    summed = sum((jnp.pad(framed[:, quarter * stride:(quarter + 1) * stride], ((quarter, 3 - quarter), (0, 0))) for quarter in range(4)))
    return summed[:frame_count].reshape(frame_count * stride)

def one_clip(spectrum, recorded, length):
    synthesis = wave_table(jnp.arange(2 * BINS).astype(jnp.int32)[:, None], jnp.arange(NFFT).astype(jnp.int32)[None, :], NFFT, 1.0 / math.sqrt(BINS))
    stacked = spectrum.reshape(2 * BINS, FRAMES)
    signals = jnp.dot(stacked.T, synthesis, preferred_element_type=jnp.float32)
    sample_index = jnp.arange(SAMPLES).astype(jnp.int32)
    inside = sample_index < length * HOP
    estimate = jnp.where(inside, intersection_rows(signals, NFFT), 0.0).astype(jnp.bfloat16)
    clean = jnp.where(inside, recorded, jnp.zeros_like(recorded))
    clip_terms = []
    gradient = jnp.zeros((SAMPLES,), jnp.float32)
    for points in (NFFT // 4, NFFT // 2, NFFT):
        stride = points // 4
        halfway = points // 2
        analysis = wave_table(jnp.arange(points).astype(jnp.int32)[None, :], jnp.arange(points).astype(jnp.int32)[:, None], points, 1.0 / math.sqrt(points))
        est_x = jnp.dot(frame_rows(estimate, points), analysis, preferred_element_type=jnp.float32)
        tgt_x = jnp.dot(frame_rows(clean, points), analysis, preferred_element_type=jnp.float32)
        est_real = est_x[:, :halfway]
        est_imag = est_x[:, halfway:]
        est_mag = jnp.sqrt(est_real * est_real + est_imag * est_imag + EPS_MAG)
        tgt_mag = jnp.sqrt(tgt_x[:, :halfway] * tgt_x[:, :halfway] + tgt_x[:, halfway:] * tgt_x[:, halfway:] + EPS_MAG)
        usable_count = length * (HOP // stride)
        usable = (jnp.arange(SAMPLES // stride).astype(jnp.int32) < usable_count)[:, None]
        mag_gap = est_mag - tgt_mag
        log_gap = jnp.log(est_mag) - jnp.log(tgt_mag)
        spread = jnp.sum(jnp.where(usable, mag_gap * mag_gap, 0.0))
        energy = jnp.sum(jnp.where(usable, tgt_mag * tgt_mag, 0.0))
        entries = (usable_count * halfway).astype(jnp.float32)
        logterm = jnp.sum(jnp.where(usable, log_gap * log_gap, 0.0)) / entries
        clip_terms.append(jnp.sqrt((spread + EPS_RATIO) / energy) + logterm)
        grad_mag = jnp.where(usable, mag_gap / jnp.sqrt((spread + EPS_RATIO) * energy) + 2.0 * log_gap / (est_mag * entries), 0.0) * (FRAMES * BINS)
        grad_x = jnp.concatenate([grad_mag * est_real / est_mag, grad_mag * est_imag / est_mag], axis=1).astype(jnp.bfloat16)
        grad_frames = jnp.dot(grad_x, analysis.T, preferred_element_type=jnp.float32)
        gradient = gradient + intersection_rows(grad_frames, points)
    grad_wave = jnp.where(inside, gradient, 0.0).astype(jnp.bfloat16)
    hop_rows = jnp.concatenate([grad_wave.reshape(FRAMES, HOP), jnp.zeros((3, HOP), jnp.bfloat16)], axis=0)
    grad_signals = jnp.concatenate([hop_rows[quarter:quarter + FRAMES] for quarter in range(4)], axis=1)
    spec_grad = jnp.dot(grad_signals, synthesis.T, preferred_element_type=jnp.float32).T.reshape(2, BINS, FRAMES).astype(jnp.bfloat16)
    return (sum(clip_terms), spec_grad)

def reference(spectra, target, lengths):

    def per_clip(clip_items):
        return one_clip(clip_items[0], clip_items[1], clip_items[2])
    losses, spec_grad = lax.map(per_clip, (spectra, target, lengths))
    return (jnp.sum(losses) / (3 * CLIPS), spec_grad)
```

```python
import math

import jax
import jax.numpy as jnp
from jax import lax
from jax.sharding import PartitionSpec as P

BINS = 1024
NFFT = 2048
HOP = 512


EPS_MAG = 0.1
EPS_RATIO = 1e-05


def shifted(block, axis, distance):
    devices = range(lax.axis_size(axis))
    route = [(i - distance, i) for i in devices if i - distance in devices]
    return lax.ppermute(block, axis, route)


def angle_pair(index, points):
    angles = (index % points).astype(jnp.float32) * (2.0 * math.pi / points)
    return jnp.cos(angles), jnp.sin(angles)


def window_of(time_index, points):
    return 0.5 - 0.5 * jnp.cos(time_index.astype(jnp.float32) * (2.0 * math.pi / points))


def analysis_table(points):
    halfway = points // 2
    lanes = min(128, halfway)
    groups = halfway // lanes
    time_index = jnp.arange(points, dtype=jnp.int32)[:, None]
    coarse_cos, coarse_sin = angle_pair(
        (jnp.arange(groups, dtype=jnp.int32)[None, :] * lanes) * time_index, points
    )
    fine_cos, fine_sin = angle_pair(jnp.arange(lanes, dtype=jnp.int32)[None, :] * time_index, points)
    cos_full = (
        coarse_cos[:, :, None] * fine_cos[:, None, :] - coarse_sin[:, :, None] * fine_sin[:, None, :]
    )
    sin_full = (
        coarse_sin[:, :, None] * fine_cos[:, None, :] + coarse_cos[:, :, None] * fine_sin[:, None, :]
    )
    window = window_of(time_index, points)[:, :, None]
    factor = 1.0 / math.sqrt(points)
    real = (cos_full * window * factor).astype(jnp.bfloat16).reshape(points, halfway)
    imag = (-sin_full * window * factor).astype(jnp.bfloat16).reshape(points, halfway)
    return jnp.concatenate([real, imag], axis=1)


def synthesis_rows(first_bin, band_count):
    sub = 8 if band_count % 8 == 0 else 1
    time_index = jnp.arange(NFFT, dtype=jnp.int32)[None, :]
    coarse_bins = first_bin + sub * jnp.arange(band_count // sub, dtype=jnp.int32)[:, None]
    coarse_cos, coarse_sin = angle_pair(coarse_bins * time_index, NFFT)
    fine_cos, fine_sin = angle_pair(jnp.arange(sub, dtype=jnp.int32)[:, None] * time_index, NFFT)
    cos_full = (
        coarse_cos[:, None, :] * fine_cos[None, :, :] - coarse_sin[:, None, :] * fine_sin[None, :, :]
    )
    sin_full = (
        coarse_sin[:, None, :] * fine_cos[None, :, :] + coarse_cos[:, None, :] * fine_sin[None, :, :]
    )
    window = window_of(time_index, NFFT)[None, :, :]
    factor = 1.0 / math.sqrt(BINS)
    real = (cos_full * window * factor).astype(jnp.bfloat16).reshape(band_count, NFFT)
    imag = (-sin_full * window * factor).astype(jnp.bfloat16).reshape(band_count, NFFT)
    return jnp.stack([real, imag])


def spread_parts(quarters):
    return sum(
        (
            jnp.pad(quarters[:, :, quarter], ((0, 0), (quarter, 3 - quarter), (0, 0)))
            for quarter in range(4)
        )
    )


def framed(signal, beyond, stride):
    frame_count = signal.shape[1] // stride
    padded = jnp.concatenate([signal, beyond], axis=1).reshape(
        signal.shape[0], frame_count + 3, stride
    )
    return jnp.concatenate(
        [padded[:, quarter : quarter + frame_count] for quarter in range(4)], axis=2
    )


def body(spectra, target, lengths):
    clip_count = spectra.shape[0]
    band_count = spectra.shape[2]
    frames_all = spectra.shape[3]
    samples = target.shape[1]
    rows_here = samples // HOP
    seg_index = lax.axis_index("seg")
    start_sample = seg_index * samples
    local_table = synthesis_rows(seg_index * band_count, band_count)
    padded_spec = jnp.pad(spectra, ((0, 0), (0, 0), (0, 0), (3, 0)))
    framed_sig = jnp.einsum(
        "crbf,rbm->fcm", padded_spec, local_table, preferred_element_type=jnp.float32
    )
    hop_rows = lax.psum_scatter(
        sum(
            (
                framed_sig[
                    3 - quarter : 3 - quarter + rows_here * lax.axis_size("seg"),
                    :,
                    quarter * HOP : (quarter + 1) * HOP,
                ]
                for quarter in range(4)
            )
        ),
        "seg",
        scatter_dimension=0,
        tiled=True,
    )
    estimate = jnp.transpose(hop_rows, (1, 0, 2)).reshape(clip_count, samples)
    sample_index = start_sample + jnp.arange(samples, dtype=jnp.int32)
    inside = sample_index[None, :] < (lengths * HOP)[:, None]
    est_wave = jnp.where(inside, estimate, 0.0).astype(jnp.bfloat16)
    clean = jnp.where(inside, target, jnp.zeros_like(target))
    sizes_list = (NFFT // 4, NFFT // 2, NFFT)
    beyond_list = [
        shifted((est_wave[:, : 3 * NFFT // 16], clean[:, : 3 * NFFT // 16]), "seg", -1),
        shifted((est_wave[:, : 3 * NFFT // 8], clean[:, : 3 * NFFT // 8]), "seg", -1),
        shifted((est_wave[:, : 3 * NFFT // 4], clean[:, : 3 * NFFT // 4]), "seg", -1),
    ]
    saved = []
    spread_list = []
    energy_list = []
    logterm_list = []
    for points, beyond_pair in zip(sizes_list, beyond_list):
        stride = points // 4
        halfway = points // 2
        frame_count = samples // stride
        paired = jnp.stack(
            [framed(est_wave, beyond_pair[0], stride), framed(clean, beyond_pair[1], stride)]
        )
        table = analysis_table(points)
        spectra_pair = jnp.einsum(
            "ecfm,mj->ecfj", paired, table, preferred_element_type=jnp.float32
        )
        est_real = spectra_pair[0, :, :, :halfway]
        est_imag = spectra_pair[0, :, :, halfway:]
        tgt_real = spectra_pair[1, :, :, :halfway]
        tgt_imag = spectra_pair[1, :, :, halfway:]
        est_mag = jnp.sqrt(est_real * est_real + est_imag * est_imag + EPS_MAG)
        tgt_mag = jnp.sqrt(tgt_real * tgt_real + tgt_imag * tgt_imag + EPS_MAG)
        usable_count = lengths * (HOP // stride)
        frame_index = start_sample // stride + jnp.arange(frame_count, dtype=jnp.int32)
        usable = frame_index[None, :, None] < usable_count[:, None, None]
        mag_gap = est_mag - tgt_mag
        log_gap = jnp.log(est_mag) - jnp.log(tgt_mag)
        entries = (usable_count * halfway).astype(jnp.float32)
        spread_list.append(jnp.sum(jnp.where(usable, mag_gap * mag_gap, 0.0), axis=(1, 2)))
        energy_list.append(jnp.sum(jnp.where(usable, tgt_mag * tgt_mag, 0.0), axis=(1, 2)))
        logterm_list.append(
            jnp.sum(jnp.where(usable, log_gap * log_gap, 0.0), axis=(1, 2)) / entries
        )
        saved.append((est_real, est_imag, est_mag, mag_gap, log_gap, usable, entries, table))
    spreads = jnp.stack(spread_list)
    energies = jnp.stack(energy_list)
    logterms = jnp.stack(logterm_list)
    spreads, energies, logterms = lax.psum((spreads, energies, logterms), "seg")
    own_loss = jnp.sum(jnp.sqrt((spreads + EPS_RATIO) / energies) + logterms)
    loss = lax.psum(own_loss, "clip") / (3 * clip_count * lax.axis_size("clip"))
    ratio_weight = 1.0 / jnp.sqrt((spreads + EPS_RATIO) * energies)
    gradient = jnp.zeros((clip_count, samples), jnp.float32)
    extras = []
    for level, points in enumerate(sizes_list):
        stride = points // 4
        frame_count = samples // stride
        est_real, est_imag, est_mag, mag_gap, log_gap, usable, entries, table = saved[level]
        grad_mag = jnp.where(
            usable,
            mag_gap * ratio_weight[level][:, None, None]
            + 2.0 * log_gap / (est_mag * entries[:, None, None]),
            0.0,
        ) * (frames_all * BINS)
        grad_x = jnp.concatenate(
            [grad_mag * est_real / est_mag, grad_mag * est_imag / est_mag], axis=2
        ).astype(jnp.bfloat16)
        grad_frames = jnp.einsum(
            "cfj,mj->cfm", grad_x, table, preferred_element_type=jnp.float32
        )
        spread_back = spread_parts(grad_frames.reshape(clip_count, frame_count, 4, stride))
        gradient = gradient + spread_back[:, :frame_count].reshape(clip_count, samples)
        extras.append(spread_back[:, frame_count:].reshape(clip_count, 3 * stride))
    received_short = shifted(extras[0], "seg", 1)
    received_middle = shifted(extras[1], "seg", 1)
    received_long = shifted(extras[2], "seg", 1)
    for received in (received_short, received_middle, received_long):
        gradient = gradient + jnp.pad(received, ((0, 0), (0, samples - received.shape[1])))
    grad_wave = jnp.where(inside, gradient, 0.0).astype(jnp.bfloat16)
    grad_hops = grad_wave.reshape(clip_count, rows_here, HOP)
    initial = jnp.zeros((clip_count, 2, band_count, frames_all + 3), jnp.float32)
    running = initial
    portion = lax.all_gather(grad_hops, "seg", axis=1, tiled=True)
    first_row = jnp.int32(0)
    for quarter in range(4):
        contrib = jnp.einsum(
            "cjm,rbm->crbj",
            portion,
            local_table[:, :, quarter * HOP : (quarter + 1) * HOP],
            preferred_element_type=jnp.float32,
        )
        offset = first_row + 3 - quarter
        current = lax.dynamic_slice_in_dim(running, offset, portion.shape[1], 3)
        running = lax.dynamic_update_slice_in_dim(running, current + contrib, offset, 3)
    spec_grad = running[:, :, :, 3:].astype(jnp.bfloat16)
    return (loss, spec_grad)


def solution(mesh):
    return jax.shard_map(
        body,
        mesh=mesh,
        in_specs=(P("clip", None, "seg", None), P("clip", "seg"), P("clip")),
        out_specs=(P(), P("clip", None, "seg", None)),
        check_vma=False,
    )
```

```python
import math

import jax
import jax.numpy as jnp
from jax import lax
from jax.sharding import PartitionSpec as P

BINS = 1024
NFFT = 2048
HOP = 512


EPS_MAG = 0.1
EPS_RATIO = 1e-05


def shifted(block, axis, distance):
    devices = range(lax.axis_size(axis))
    route = [(i - distance, i) for i in devices if i - distance in devices]
    return lax.ppermute(block, axis, route)


def angle_pair(index, points):
    angles = (index % points).astype(jnp.float32) * (2.0 * math.pi / points)
    return jnp.cos(angles), jnp.sin(angles)


def window_of(time_index, points):
    return 0.5 - 0.5 * jnp.cos(time_index.astype(jnp.float32) * (2.0 * math.pi / points))


def analysis_table(points, fine):
    halfway = points // 2
    lanes = fine[0].shape[1]
    groups = halfway // lanes
    time_index = jnp.arange(points, dtype=jnp.int32)[:, None]
    coarse_cos, coarse_sin = angle_pair(
        (jnp.arange(groups, dtype=jnp.int32)[None, :] * lanes) * time_index, points
    )
    first = jnp.concatenate([coarse_cos, -coarse_sin], axis=1)
    second = jnp.concatenate([-coarse_sin, -coarse_cos], axis=1)
    fine_cos, fine_sin = fine
    window = window_of(time_index, points)[:, :, None]
    entry_value = first[:, :, None] * fine_cos[:, None, :] + second[:, :, None] * fine_sin[:, None, :]
    return (entry_value * window * (1.0 / math.sqrt(points))).astype(jnp.bfloat16).reshape(
        points, points
    )


def synthesis_rows(first_bin, band_count):
    sub = 8 if band_count % 8 == 0 else 1
    time_index = jnp.arange(NFFT, dtype=jnp.int32)[None, :]
    coarse_bins = first_bin + sub * jnp.arange(band_count // sub, dtype=jnp.int32)[:, None]
    coarse_cos, coarse_sin = angle_pair(coarse_bins * time_index, NFFT)
    fine_cos, fine_sin = angle_pair(jnp.arange(sub, dtype=jnp.int32)[:, None] * time_index, NFFT)
    first = jnp.stack([coarse_cos, -coarse_sin])
    second = jnp.stack([-coarse_sin, -coarse_cos])
    window = window_of(time_index, NFFT)[None, None, :, :]
    entry_value = (
        first[:, :, None, :] * fine_cos[None, None, :, :]
        + second[:, :, None, :] * fine_sin[None, None, :, :]
    )
    return (entry_value * window * (1.0 / math.sqrt(BINS))).astype(jnp.bfloat16).reshape(
        2, band_count, NFFT
    )


def spread_parts(quarters):
    return sum(
        (
            jnp.pad(quarters[:, :, quarter], ((0, 0), (quarter, 3 - quarter), (0, 0)))
            for quarter in range(4)
        )
    )


def framed(signal, beyond, stride):
    frame_count = signal.shape[1] // stride
    padded = jnp.concatenate([signal, beyond], axis=1).reshape(
        signal.shape[0], frame_count + 3, stride
    )
    return jnp.concatenate(
        [padded[:, quarter : quarter + frame_count] for quarter in range(4)], axis=2
    )


def body(spectra, target, lengths):
    clip_count = spectra.shape[0]
    band_count = spectra.shape[2]
    frames_all = spectra.shape[3]
    samples = target.shape[1]
    rows_here = samples // HOP
    seg_index = lax.axis_index("seg")
    start_sample = seg_index * samples
    local_table = synthesis_rows(seg_index * band_count, band_count)
    padded_spec = jnp.pad(spectra, ((0, 0), (0, 0), (0, 0), (3, 0)))
    framed_sig = jnp.einsum(
        "crbf,rbm->fcm", padded_spec, local_table, preferred_element_type=jnp.float32
    )
    hop_rows = lax.psum_scatter(
        sum(
            (
                framed_sig[
                    3 - quarter : 3 - quarter + rows_here * lax.axis_size("seg"),
                    :,
                    quarter * HOP : (quarter + 1) * HOP,
                ]
                for quarter in range(4)
            )
        ),
        "seg",
        scatter_dimension=0,
        tiled=True,
    )
    estimate = jnp.transpose(hop_rows, (1, 0, 2)).reshape(clip_count, samples)
    sample_index = start_sample + jnp.arange(samples, dtype=jnp.int32)
    inside = sample_index[None, :] < (lengths * HOP)[:, None]
    est_wave = jnp.where(inside, estimate, 0.0).astype(jnp.bfloat16)
    clean = jnp.where(inside, target, jnp.zeros_like(target))
    sizes_list = (NFFT // 4, NFFT // 2, NFFT)
    halo = 3 * NFFT // 4
    beyond_all = shifted(jnp.stack([est_wave[:, :halo], clean[:, :halo]]), "seg", -1)
    beyond_list = [beyond_all[:, :, : 3 * points // 4] for points in sizes_list]
    lanes = min(128, NFFT // 4)
    fine_all = angle_pair(
        jnp.arange(lanes, dtype=jnp.int32)[None, :] * jnp.arange(NFFT, dtype=jnp.int32)[:, None], NFFT
    )
    saved = []
    spread_list = []
    energy_list = []
    logterm_list = []
    for points, beyond_pair in zip(sizes_list, beyond_list):
        stride = points // 4
        halfway = points // 2
        frame_count = samples // stride
        paired = jnp.stack(
            [framed(est_wave, beyond_pair[0], stride), framed(clean, beyond_pair[1], stride)]
        )
        step = NFFT // points
        table = analysis_table(points, (fine_all[0][::step], fine_all[1][::step]))
        spectra_pair = jnp.einsum(
            "ecfm,mj->ecfj", paired, table, preferred_element_type=jnp.float32
        )
        est_real = spectra_pair[0, :, :, :halfway]
        est_imag = spectra_pair[0, :, :, halfway:]
        tgt_real = spectra_pair[1, :, :, :halfway]
        tgt_imag = spectra_pair[1, :, :, halfway:]
        est_mag = jnp.sqrt(est_real * est_real + est_imag * est_imag + EPS_MAG)
        tgt_mag = jnp.sqrt(tgt_real * tgt_real + tgt_imag * tgt_imag + EPS_MAG)
        usable_count = lengths * (HOP // stride)
        frame_index = start_sample // stride + jnp.arange(frame_count, dtype=jnp.int32)
        usable = frame_index[None, :, None] < usable_count[:, None, None]
        mag_gap = est_mag - tgt_mag
        log_gap = jnp.log(est_mag) - jnp.log(tgt_mag)
        entries = (usable_count * halfway).astype(jnp.float32)
        spread_list.append(jnp.sum(jnp.where(usable, mag_gap * mag_gap, 0.0), axis=(1, 2)))
        energy_list.append(jnp.sum(jnp.where(usable, tgt_mag * tgt_mag, 0.0), axis=(1, 2)))
        logterm_list.append(
            jnp.sum(jnp.where(usable, log_gap * log_gap, 0.0), axis=(1, 2)) / entries
        )
        saved.append((est_real, est_imag, est_mag, mag_gap, log_gap, usable, entries, table))
    spreads = jnp.stack(spread_list)
    energies = jnp.stack(energy_list)
    logterms = jnp.stack(logterm_list)
    clip_index = lax.axis_index("clip")
    clip_groups = lax.axis_size("clip")
    stats = jnp.stack([spreads, energies, logterms])
    slots = jnp.where(
        (jnp.arange(clip_groups, dtype=jnp.int32) == clip_index)[:, None, None, None],
        stats[None],
        0.0,
    )
    slots = lax.psum(slots, ("clip", "seg"))
    loss = jnp.sum(jnp.sqrt((slots[:, 0] + EPS_RATIO) / slots[:, 1]) + slots[:, 2]) / (
        3 * clip_count * clip_groups
    )
    spreads, energies, logterms = slots[clip_index]
    ratio_weight = 1.0 / jnp.sqrt((spreads + EPS_RATIO) * energies)
    gradient = jnp.zeros((clip_count, samples), jnp.float32)
    extras = []
    for level, points in enumerate(sizes_list):
        stride = points // 4
        frame_count = samples // stride
        est_real, est_imag, est_mag, mag_gap, log_gap, usable, entries, table = saved[level]
        grad_mag = jnp.where(
            usable,
            mag_gap * ratio_weight[level][:, None, None]
            + 2.0 * log_gap / (est_mag * entries[:, None, None]),
            0.0,
        ) * (frames_all * BINS)
        grad_x = jnp.concatenate(
            [grad_mag * est_real / est_mag, grad_mag * est_imag / est_mag], axis=2
        ).astype(jnp.bfloat16)
        grad_frames = jnp.einsum(
            "cfj,mj->cfm", grad_x, table, preferred_element_type=jnp.float32
        )
        spread_back = spread_parts(grad_frames.reshape(clip_count, frame_count, 4, stride))
        gradient = gradient + spread_back[:, :frame_count].reshape(clip_count, samples)
        extras.append(spread_back[:, frame_count:].reshape(clip_count, 3 * stride))
    halo = 3 * NFFT // 4
    spill = sum(jnp.pad(extra, ((0, 0), (0, halo - extra.shape[1]))) for extra in extras)
    received = shifted(spill, "seg", 1)
    gradient = gradient + jnp.pad(received, ((0, 0), (0, samples - halo)))
    grad_wave = jnp.where(inside, gradient, 0.0).astype(jnp.bfloat16)
    grad_hops = grad_wave.reshape(clip_count, rows_here, HOP)
    portion = lax.all_gather(grad_hops, "seg", axis=1, tiled=True)
    padded = jnp.concatenate([portion, jnp.zeros((clip_count, 3, HOP), portion.dtype)], axis=1)
    grad_signals = jnp.concatenate(
        [padded[:, quarter : quarter + frames_all] for quarter in range(4)], axis=2
    )
    spec_grad = jnp.einsum(
        "ctm,rbm->crbt", grad_signals, local_table, preferred_element_type=jnp.float32
    ).astype(jnp.bfloat16)
    return (loss, spec_grad)


def solution(mesh):
    return jax.shard_map(
        body,
        mesh=mesh,
        in_specs=(P("clip", None, "seg", None), P("clip", "seg"), P("clip")),
        out_specs=(P(), P("clip", None, "seg", None)),
        check_vma=False,
    )
```

```python
import math

import jax
import jax.numpy as jnp
from jax import lax
from jax.sharding import PartitionSpec as P

BINS = 1024
NFFT = 2048
HOP = 512


EPS_MAG = 0.1
EPS_RATIO = 1e-05


def shifted(block, axis, distance):
    devices = range(lax.axis_size(axis))
    route = [(i - distance, i) for i in devices if i - distance in devices]
    return lax.ppermute(block, axis, route)


def angle_pair(index, points):
    angles = (index % points).astype(jnp.float32) * (2.0 * math.pi / points)
    return jnp.cos(angles), jnp.sin(angles)


def window_of(time_index, points):
    return 0.5 - 0.5 * jnp.cos(time_index.astype(jnp.float32) * (2.0 * math.pi / points))


def analysis_table(points, fine):
    halfway = points // 2
    lanes = fine[0].shape[0]
    groups = halfway // lanes
    time_index = jnp.arange(points, dtype=jnp.int32)[None, :]
    row = jnp.arange(2 * groups, dtype=jnp.int32)[:, None]
    is_sine = row >= groups
    coarse_cos, coarse_sin = angle_pair(((row % groups) * lanes) * time_index, points)
    first = jnp.where(is_sine, -coarse_sin, coarse_cos)
    second = jnp.where(is_sine, -coarse_cos, -coarse_sin)
    scale = window_of(time_index, points) * (1.0 / math.sqrt(points))
    fine_cos, fine_sin = (part * scale for part in fine)
    entry_value = first[:, None, :] * fine_cos[None, :, :] + second[:, None, :] * fine_sin[None, :, :]
    table = entry_value.astype(jnp.bfloat16)
    return lax.optimization_barrier(table.reshape(points, points))


def synthesis_rows(first_bin, band_count):
    sub = 16 if band_count % 16 == 0 else 1
    time_index = jnp.arange(NFFT, dtype=jnp.int32)[None, :]
    row = jnp.arange(2 * (band_count // sub), dtype=jnp.int32)[:, None]
    is_sine = row >= band_count // sub
    coarse_bins = first_bin + sub * (row % (band_count // sub))
    coarse_cos, coarse_sin = angle_pair(coarse_bins * time_index, NFFT)
    scale = window_of(time_index, NFFT) * (1.0 / math.sqrt(BINS))
    fine_cos, fine_sin = (
        part * scale
        for part in angle_pair(jnp.arange(sub, dtype=jnp.int32)[:, None] * time_index, NFFT)
    )
    first = jnp.where(is_sine, -coarse_sin, coarse_cos)
    second = jnp.where(is_sine, -coarse_cos, -coarse_sin)
    entry_value = first[:, None, :] * fine_cos[None, :, :] + second[:, None, :] * fine_sin[None, :, :]
    table = entry_value.astype(jnp.bfloat16)
    return lax.optimization_barrier(table.reshape(2, band_count, NFFT))


def gathered_sum(value, axis):
    size = lax.axis_size(axis)
    here = lax.axis_index(axis)
    devices = range(size)
    slots = jnp.zeros((size,) + value.shape, value.dtype)
    for distance in range(size):
        if distance == 0:
            arrived = value
        else:
            route = [(i, (i + distance) % size) for i in devices]
            arrived = lax.ppermute(value, axis, route)
        source = (here - distance) % size
        slots = slots + jnp.where(
            (jnp.arange(size, dtype=jnp.int32) == source).reshape((size,) + (1,) * value.ndim),
            arrived[None],
            0.0,
        )
    return jnp.sum(slots, axis=0)


def spread_parts(quarters):
    return sum(
        (
            jnp.pad(quarters[:, :, quarter], ((0, 0), (quarter, 3 - quarter), (0, 0)))
            for quarter in range(4)
        )
    )


def framed(signal, beyond, stride):
    frame_count = signal.shape[1] // stride
    padded = jnp.concatenate([signal, beyond], axis=1).reshape(
        signal.shape[0], frame_count + 3, stride
    )
    return jnp.concatenate(
        [padded[:, quarter : quarter + frame_count] for quarter in range(4)], axis=2
    )


def body(spectra, target, lengths):
    clip_count = spectra.shape[0]
    band_count = spectra.shape[2]
    frames_all = spectra.shape[3]
    samples = target.shape[1]
    rows_here = samples // HOP
    seg_index = lax.axis_index("seg")
    start_sample = seg_index * samples
    local_table = synthesis_rows(seg_index * band_count, band_count)
    padded_spec = jnp.pad(spectra, ((0, 0), (0, 0), (0, 0), (3, 0)))
    framed_sig = jnp.einsum(
        "crbf,rbm->fcm", padded_spec, local_table, preferred_element_type=jnp.float32
    )
    hop_rows = lax.psum_scatter(
        sum(
            (
                framed_sig[
                    3 - quarter : 3 - quarter + rows_here * lax.axis_size("seg"),
                    :,
                    quarter * HOP : (quarter + 1) * HOP,
                ]
                for quarter in range(4)
            )
        ),
        "seg",
        scatter_dimension=0,
        tiled=True,
    )
    estimate = jnp.transpose(hop_rows, (1, 0, 2)).reshape(clip_count, samples)
    sample_index = start_sample + jnp.arange(samples, dtype=jnp.int32)
    inside = sample_index[None, :] < (lengths * HOP)[:, None]
    est_wave = jnp.where(inside, estimate, 0.0).astype(jnp.bfloat16)
    clean = jnp.where(inside, target, jnp.zeros_like(target))
    sizes_list = (NFFT // 4, NFFT // 2, NFFT)
    halo = 3 * NFFT // 4
    beyond_all = shifted(jnp.stack([est_wave[:, :halo], clean[:, :halo]]), "seg", -1)
    beyond_list = [beyond_all[:, :, : 3 * points // 4] for points in sizes_list]
    lanes = min(128, NFFT // 4)
    fine_all = angle_pair(
        jnp.arange(lanes, dtype=jnp.int32)[:, None] * jnp.arange(NFFT, dtype=jnp.int32)[None, :], NFFT
    )
    saved = []
    spread_list = []
    energy_list = []
    logterm_list = []
    for points, beyond_pair in zip(sizes_list, beyond_list):
        stride = points // 4
        halfway = points // 2
        frame_count = samples // stride
        paired = jnp.stack(
            [framed(est_wave, beyond_pair[0], stride), framed(clean, beyond_pair[1], stride)]
        )
        step = NFFT // points
        table = analysis_table(points, (fine_all[0][:, ::step], fine_all[1][:, ::step]))
        spectra_pair = jnp.einsum(
            "ecfm,jm->ecfj", paired, table, preferred_element_type=jnp.float32
        )
        est_real = spectra_pair[0, :, :, :halfway]
        est_imag = spectra_pair[0, :, :, halfway:]
        tgt_real = spectra_pair[1, :, :, :halfway]
        tgt_imag = spectra_pair[1, :, :, halfway:]
        est_mag = jnp.sqrt(est_real * est_real + est_imag * est_imag + EPS_MAG)
        tgt_mag = jnp.sqrt(tgt_real * tgt_real + tgt_imag * tgt_imag + EPS_MAG)
        usable_count = lengths * (HOP // stride)
        frame_index = start_sample // stride + jnp.arange(frame_count, dtype=jnp.int32)
        usable = frame_index[None, :, None] < usable_count[:, None, None]
        mag_gap = est_mag - tgt_mag
        log_gap = jnp.log(est_mag) - jnp.log(tgt_mag)
        entries = (usable_count * halfway).astype(jnp.float32)
        spread_list.append(jnp.sum(jnp.where(usable, mag_gap * mag_gap, 0.0), axis=(1, 2)))
        energy_list.append(jnp.sum(jnp.where(usable, tgt_mag * tgt_mag, 0.0), axis=(1, 2)))
        logterm_list.append(
            jnp.sum(jnp.where(usable, log_gap * log_gap, 0.0), axis=(1, 2)) / entries
        )
        saved.append((est_real, est_imag, est_mag, mag_gap, log_gap, usable, entries, table))
    spreads = jnp.stack(spread_list)
    energies = jnp.stack(energy_list)
    logterms = jnp.stack(logterm_list)
    spreads, energies, logterms = lax.psum((spreads, energies, logterms), "seg")
    own_loss = jnp.sum(jnp.sqrt((spreads + EPS_RATIO) / energies) + logterms)
    loss = gathered_sum(own_loss, "clip") / (3 * clip_count * lax.axis_size("clip"))
    ratio_weight = 1.0 / jnp.sqrt((spreads + EPS_RATIO) * energies)
    gradient = jnp.zeros((clip_count, samples), jnp.float32)
    extras = []
    for level, points in enumerate(sizes_list):
        stride = points // 4
        frame_count = samples // stride
        est_real, est_imag, est_mag, mag_gap, log_gap, usable, entries, table = saved[level]
        grad_mag = jnp.where(
            usable,
            mag_gap * ratio_weight[level][:, None, None]
            + 2.0 * log_gap / (est_mag * entries[:, None, None]),
            0.0,
        ) * (frames_all * BINS)
        grad_x = jnp.concatenate(
            [grad_mag * est_real / est_mag, grad_mag * est_imag / est_mag], axis=2
        ).astype(jnp.bfloat16)
        grad_frames = jnp.einsum(
            "cfj,jm->cfm", grad_x, table, preferred_element_type=jnp.float32
        )
        spread_back = spread_parts(grad_frames.reshape(clip_count, frame_count, 4, stride))
        gradient = gradient + spread_back[:, :frame_count].reshape(clip_count, samples)
        extras.append(spread_back[:, frame_count:].reshape(clip_count, 3 * stride))
    halo = 3 * NFFT // 4
    spill = sum(jnp.pad(extra, ((0, 0), (0, halo - extra.shape[1]))) for extra in extras)
    received = shifted(spill, "seg", 1)
    gradient = gradient + jnp.pad(received, ((0, 0), (0, samples - halo)))
    grad_wave = jnp.where(inside, gradient, 0.0).astype(jnp.bfloat16)
    grad_hops = grad_wave.reshape(clip_count, rows_here, HOP)
    portion = lax.all_gather(grad_hops, "seg", axis=1, tiled=True)
    padded = jnp.concatenate([portion, jnp.zeros((clip_count, 3, HOP), portion.dtype)], axis=1)
    grad_signals = jnp.concatenate(
        [padded[:, quarter : quarter + frames_all] for quarter in range(4)], axis=2
    )
    spec_grad = jnp.einsum(
        "ctm,rbm->crbt", grad_signals, local_table, preferred_element_type=jnp.float32
    ).astype(jnp.bfloat16)
    return (loss, spec_grad)


def solution(mesh):
    return jax.shard_map(
        body,
        mesh=mesh,
        in_specs=(P("clip", None, "seg", None), P("clip", "seg"), P("clip")),
        out_specs=(P(), P("clip", None, "seg", None)),
        check_vma=False,
    )
```

```python
import math

import jax
import jax.numpy as jnp
from jax import lax
from jax.sharding import PartitionSpec as P

BINS = 1024
NFFT = 2048
HOP = 512


EPS_MAG = 0.1
EPS_RATIO = 1e-05


def shifted(block, axis, distance):
    devices = range(lax.axis_size(axis))
    route = [(i - distance, i) for i in devices if i - distance in devices]
    return lax.ppermute(block, axis, route)


def angle_pair(index, points):
    angles = (index % points).astype(jnp.float32) * (2.0 * math.pi / points)
    return jnp.cos(angles), jnp.sin(angles)


def window_of(time_index, points):
    return 0.5 - 0.5 * jnp.cos(time_index.astype(jnp.float32) * (2.0 * math.pi / points))


def analysis_table(points):
    halfway = points // 2
    lanes = min(128, halfway)
    groups = halfway // lanes
    time_index = jnp.arange(points, dtype=jnp.int32)[None, :]
    fine = angle_pair(jnp.arange(lanes, dtype=jnp.int32)[:, None] * time_index, points)
    row = jnp.arange(2 * groups, dtype=jnp.int32)[:, None]
    is_sine = row >= groups
    coarse_cos, coarse_sin = angle_pair(((row % groups) * lanes) * time_index, points)
    first = jnp.where(is_sine, -coarse_sin, coarse_cos)
    second = jnp.where(is_sine, -coarse_cos, -coarse_sin)
    scale = window_of(time_index, points) * (1.0 / math.sqrt(points))
    fine_cos, fine_sin = (part * scale for part in fine)
    entry_value = first[:, None, :] * fine_cos[None, :, :] + second[:, None, :] * fine_sin[None, :, :]
    table = entry_value.astype(jnp.bfloat16)
    return lax.optimization_barrier(table.reshape(points, points))


def synthesis_rows(first_bin, band_count):
    sub = 16 if band_count % 16 == 0 else 1
    time_index = jnp.arange(NFFT, dtype=jnp.int32)[None, :]
    row = jnp.arange(2 * (band_count // sub), dtype=jnp.int32)[:, None]
    is_sine = row >= band_count // sub
    coarse_bins = first_bin + sub * (row % (band_count // sub))
    coarse_cos, coarse_sin = angle_pair(coarse_bins * time_index, NFFT)
    scale = window_of(time_index, NFFT) * (1.0 / math.sqrt(BINS))
    fine_cos, fine_sin = (
        part * scale
        for part in angle_pair(jnp.arange(sub, dtype=jnp.int32)[:, None] * time_index, NFFT)
    )
    first = jnp.where(is_sine, -coarse_sin, coarse_cos)
    second = jnp.where(is_sine, -coarse_cos, -coarse_sin)
    entry_value = first[:, None, :] * fine_cos[None, :, :] + second[:, None, :] * fine_sin[None, :, :]
    table = entry_value.astype(jnp.bfloat16)
    return lax.optimization_barrier(table.reshape(2, band_count, NFFT))


def gathered_sum(value, axis):
    size = lax.axis_size(axis)
    here = lax.axis_index(axis)
    devices = range(size)
    slots = jnp.zeros((size,) + value.shape, value.dtype)
    for distance in range(size):
        if distance == 0:
            arrived = value
        else:
            route = [(i, (i + distance) % size) for i in devices]
            arrived = lax.ppermute(value, axis, route)
        source = (here - distance) % size
        slots = slots + jnp.where(
            (jnp.arange(size, dtype=jnp.int32) == source).reshape((size,) + (1,) * value.ndim),
            arrived[None],
            0.0,
        )
    return jnp.sum(slots, axis=0)


def spread_parts(quarters):
    return sum(
        (
            jnp.pad(quarters[:, :, quarter], ((0, 0), (quarter, 3 - quarter), (0, 0)))
            for quarter in range(4)
        )
    )


def framed(signal, beyond, stride):
    frame_count = signal.shape[1] // stride
    padded = jnp.concatenate([signal, beyond], axis=1).reshape(
        signal.shape[0], frame_count + 3, stride
    )
    return jnp.concatenate(
        [padded[:, quarter : quarter + frame_count] for quarter in range(4)], axis=2
    )


def body(spectra, target, lengths):
    clip_count = spectra.shape[0]
    band_count = spectra.shape[2]
    frames_all = spectra.shape[3]
    samples = target.shape[1]
    rows_here = samples // HOP
    seg_index = lax.axis_index("seg")
    start_sample = seg_index * samples
    local_table = synthesis_rows(seg_index * band_count, band_count)
    padded_spec = jnp.pad(spectra, ((0, 0), (0, 0), (0, 0), (3, 0)))
    framed_sig = jnp.einsum(
        "crbf,rbm->fcm", padded_spec, local_table, preferred_element_type=jnp.float32
    )
    hop_rows = lax.psum_scatter(
        sum(
            (
                framed_sig[
                    3 - quarter : 3 - quarter + rows_here * lax.axis_size("seg"),
                    :,
                    quarter * HOP : (quarter + 1) * HOP,
                ]
                for quarter in range(4)
            )
        ),
        "seg",
        scatter_dimension=0,
        tiled=True,
    )
    estimate = jnp.transpose(hop_rows, (1, 0, 2)).reshape(clip_count, samples)
    sample_index = start_sample + jnp.arange(samples, dtype=jnp.int32)
    inside = sample_index[None, :] < (lengths * HOP)[:, None]
    est_wave = jnp.where(inside, estimate, 0.0).astype(jnp.bfloat16)
    clean = jnp.where(inside, target, jnp.zeros_like(target))
    sizes_list = (NFFT // 4, NFFT // 2, NFFT)
    halo = 3 * NFFT // 4
    beyond_all = shifted(jnp.stack([est_wave[:, :halo], clean[:, :halo]]), "seg", -1)
    beyond_list = [beyond_all[:, :, : 3 * points // 4] for points in sizes_list]
    saved = []
    spread_list = []
    energy_list = []
    logterm_list = []
    for points, beyond_pair in zip(sizes_list, beyond_list):
        stride = points // 4
        halfway = points // 2
        frame_count = samples // stride
        paired = jnp.stack(
            [framed(est_wave, beyond_pair[0], stride), framed(clean, beyond_pair[1], stride)]
        )
        table = analysis_table(points)
        spectra_pair = jnp.einsum(
            "ecfm,jm->ecfj", paired, table, preferred_element_type=jnp.float32
        )
        est_real = spectra_pair[0, :, :, :halfway]
        est_imag = spectra_pair[0, :, :, halfway:]
        tgt_real = spectra_pair[1, :, :, :halfway]
        tgt_imag = spectra_pair[1, :, :, halfway:]
        est_mag = jnp.sqrt(est_real * est_real + est_imag * est_imag + EPS_MAG)
        tgt_mag = jnp.sqrt(tgt_real * tgt_real + tgt_imag * tgt_imag + EPS_MAG)
        usable_count = lengths * (HOP // stride)
        frame_index = start_sample // stride + jnp.arange(frame_count, dtype=jnp.int32)
        usable = frame_index[None, :, None] < usable_count[:, None, None]
        mag_gap = est_mag - tgt_mag
        log_gap = jnp.log(est_mag) - jnp.log(tgt_mag)
        entries = (usable_count * halfway).astype(jnp.float32)
        spread_list.append(jnp.sum(jnp.where(usable, mag_gap * mag_gap, 0.0), axis=(1, 2)))
        energy_list.append(jnp.sum(jnp.where(usable, tgt_mag * tgt_mag, 0.0), axis=(1, 2)))
        logterm_list.append(
            jnp.sum(jnp.where(usable, log_gap * log_gap, 0.0), axis=(1, 2)) / entries
        )
        saved.append((est_real, est_imag, est_mag, mag_gap, log_gap, usable, entries, table))
    spreads = jnp.stack(spread_list)
    energies = jnp.stack(energy_list)
    logterms = jnp.stack(logterm_list)
    spreads, energies, logterms = lax.psum((spreads, energies, logterms), "seg")
    own_loss = jnp.sum(jnp.sqrt((spreads + EPS_RATIO) / energies) + logterms)
    loss = gathered_sum(own_loss, "clip") / (3 * clip_count * lax.axis_size("clip"))
    ratio_weight = 1.0 / jnp.sqrt((spreads + EPS_RATIO) * energies)
    gradient = jnp.zeros((clip_count, samples), jnp.float32)
    extras = []
    for level, points in enumerate(sizes_list):
        stride = points // 4
        frame_count = samples // stride
        est_real, est_imag, est_mag, mag_gap, log_gap, usable, entries, table = saved[level]
        grad_mag = jnp.where(
            usable,
            mag_gap * ratio_weight[level][:, None, None]
            + 2.0 * log_gap / (est_mag * entries[:, None, None]),
            0.0,
        ) * (frames_all * BINS)
        grad_x = jnp.concatenate(
            [grad_mag * est_real / est_mag, grad_mag * est_imag / est_mag], axis=2
        ).astype(jnp.bfloat16)
        grad_frames = jnp.einsum(
            "cfj,jm->cfm", grad_x, table, preferred_element_type=jnp.float32
        )
        spread_back = spread_parts(grad_frames.reshape(clip_count, frame_count, 4, stride))
        gradient = gradient + spread_back[:, :frame_count].reshape(clip_count, samples)
        extras.append(spread_back[:, frame_count:].reshape(clip_count, 3 * stride))
    halo = 3 * NFFT // 4
    spill = sum(jnp.pad(extra, ((0, 0), (0, halo - extra.shape[1]))) for extra in extras)
    received = shifted(spill, "seg", 1)
    gradient = gradient + jnp.pad(received, ((0, 0), (0, samples - halo)))
    grad_wave = jnp.where(inside, gradient, 0.0).astype(jnp.bfloat16)
    grad_hops = grad_wave.reshape(clip_count, rows_here, HOP)
    portion = lax.all_gather(grad_hops, "seg", axis=1, tiled=True)
    padded = jnp.concatenate([portion, jnp.zeros((clip_count, 3, HOP), portion.dtype)], axis=1)
    grad_signals = jnp.concatenate(
        [padded[:, quarter : quarter + frames_all] for quarter in range(4)], axis=2
    )
    spec_grad = jnp.einsum(
        "ctm,rbm->crbt", grad_signals, local_table, preferred_element_type=jnp.float32
    ).astype(jnp.bfloat16)
    return (loss, spec_grad)


def solution(mesh):
    return jax.shard_map(
        body,
        mesh=mesh,
        in_specs=(P("clip", None, "seg", None), P("clip", "seg"), P("clip")),
        out_specs=(P(), P("clip", None, "seg", None)),
        check_vma=False,
    )
```

```python
import math

import jax
import jax.numpy as jnp
from jax import lax
from jax.sharding import PartitionSpec as P

BINS = 1024
NFFT = 2048
HOP = 512


EPS_MAG = 0.1
EPS_RATIO = 1e-05


def shifted(block, axis, distance):
    devices = range(lax.axis_size(axis))
    route = [(i - distance, i) for i in devices if i - distance in devices]
    return lax.ppermute(block, axis, route)


def angle_pair(index, points):
    angles = (index % points).astype(jnp.float32) * (2.0 * math.pi / points)
    return jnp.cos(angles), jnp.sin(angles)


def window_of(time_index, points):
    return 0.5 - 0.5 * jnp.cos(time_index.astype(jnp.float32) * (2.0 * math.pi / points))


def analysis_table(points):
    halfway = points // 2
    lanes = min(128, halfway)
    groups = halfway // lanes
    time_index = jnp.arange(points, dtype=jnp.int32)[None, :]
    fine = angle_pair(jnp.arange(lanes, dtype=jnp.int32)[:, None] * time_index, points)
    row = jnp.arange(2 * groups, dtype=jnp.int32)[:, None]
    is_sine = row >= groups
    coarse_cos, coarse_sin = angle_pair(((row % groups) * lanes) * time_index, points)
    first = jnp.where(is_sine, -coarse_sin, coarse_cos)
    second = jnp.where(is_sine, -coarse_cos, -coarse_sin)
    scale = window_of(time_index, points) * (1.0 / math.sqrt(points))
    fine_cos, fine_sin = (part * scale for part in fine)
    entry_value = first[:, None, :] * fine_cos[None, :, :] + second[:, None, :] * fine_sin[None, :, :]
    table = entry_value.astype(jnp.bfloat16)
    return lax.optimization_barrier(table.reshape(points, points))


def synthesis_rows(first_bin, band_count):
    sub = 16 if band_count % 16 == 0 else 1
    time_index = jnp.arange(NFFT, dtype=jnp.int32)[None, :]
    row = jnp.arange(2 * (band_count // sub), dtype=jnp.int32)[:, None]
    is_sine = row >= band_count // sub
    coarse_bins = first_bin + sub * (row % (band_count // sub))
    coarse_cos, coarse_sin = angle_pair(coarse_bins * time_index, NFFT)
    scale = window_of(time_index, NFFT) * (1.0 / math.sqrt(BINS))
    fine_cos, fine_sin = (
        part * scale
        for part in angle_pair(jnp.arange(sub, dtype=jnp.int32)[:, None] * time_index, NFFT)
    )
    first = jnp.where(is_sine, -coarse_sin, coarse_cos)
    second = jnp.where(is_sine, -coarse_cos, -coarse_sin)
    entry_value = first[:, None, :] * fine_cos[None, :, :] + second[:, None, :] * fine_sin[None, :, :]
    table = entry_value.astype(jnp.bfloat16)
    return lax.optimization_barrier(table.reshape(2, band_count, NFFT))


def gathered_sum(value, axis):
    size = lax.axis_size(axis)
    here = lax.axis_index(axis)
    devices = range(size)
    slots = jnp.zeros((size,) + value.shape, value.dtype)
    for distance in range(size):
        if distance == 0:
            arrived = value
        else:
            route = [(i, (i + distance) % size) for i in devices]
            arrived = lax.ppermute(value, axis, route)
        source = (here - distance) % size
        slots = slots + jnp.where(
            (jnp.arange(size, dtype=jnp.int32) == source).reshape((size,) + (1,) * value.ndim),
            arrived[None],
            0.0,
        )
    return jnp.sum(slots, axis=0)


def spread_parts(quarters):
    return sum(
        (
            jnp.pad(quarters[:, :, quarter], ((0, 0), (quarter, 3 - quarter), (0, 0)))
            for quarter in range(4)
        )
    )


def framed(signal, beyond, stride):
    frame_count = signal.shape[1] // stride
    padded = jnp.concatenate([signal, beyond], axis=1).reshape(
        signal.shape[0], frame_count + 3, stride
    )
    return jnp.concatenate(
        [padded[:, quarter : quarter + frame_count] for quarter in range(4)], axis=2
    )


def body(spectra, target, lengths):
    clip_count = spectra.shape[0]
    band_count = spectra.shape[2]
    frames_all = spectra.shape[3]
    samples = target.shape[1]
    rows_here = samples // HOP
    seg_index = lax.axis_index("seg")
    start_sample = seg_index * samples
    local_table = synthesis_rows(seg_index * band_count, band_count)
    sample_index = start_sample + jnp.arange(samples, dtype=jnp.int32)
    inside = sample_index[None, :] < (lengths * HOP)[:, None]
    clean = jnp.where(inside, target, jnp.zeros_like(target))
    clean, local_table = lax.optimization_barrier((clean, local_table))
    padded_spec = jnp.pad(spectra, ((0, 0), (0, 0), (0, 0), (3, 0)))
    framed_sig = jnp.einsum(
        "crbf,rbm->fcm", padded_spec, local_table, preferred_element_type=jnp.float32
    )
    hop_rows = lax.psum_scatter(
        sum(
            (
                framed_sig[
                    3 - quarter : 3 - quarter + rows_here * lax.axis_size("seg"),
                    :,
                    quarter * HOP : (quarter + 1) * HOP,
                ]
                for quarter in range(4)
            )
        ),
        "seg",
        scatter_dimension=0,
        tiled=True,
    )
    estimate = jnp.transpose(hop_rows, (1, 0, 2)).reshape(clip_count, samples)
    est_wave = jnp.where(inside, estimate, 0.0).astype(jnp.bfloat16)
    sizes_list = (NFFT // 4, NFFT // 2, NFFT)
    halo = 3 * NFFT // 4
    clean_beyond = shifted(clean[:, :halo], "seg", -1)
    est_beyond = shifted(est_wave[:, :halo], "seg", -1)
    saved = []
    spread_list = []
    energy_list = []
    logterm_list = []
    for points in sizes_list:
        stride = points // 4
        halfway = points // 2
        frame_count = samples // stride
        table = analysis_table(points)
        tgt_x = jnp.einsum(
            "cfm,jm->cfj",
            framed(clean, clean_beyond[:, : 3 * stride], stride),
            table,
            preferred_element_type=jnp.float32,
        )
        est_x = jnp.einsum(
            "cfm,jm->cfj",
            framed(est_wave, est_beyond[:, : 3 * stride], stride),
            table,
            preferred_element_type=jnp.float32,
        )
        est_real = est_x[:, :, :halfway]
        est_imag = est_x[:, :, halfway:]
        tgt_real = tgt_x[:, :, :halfway]
        tgt_imag = tgt_x[:, :, halfway:]
        est_mag = jnp.sqrt(est_real * est_real + est_imag * est_imag + EPS_MAG)
        tgt_mag = jnp.sqrt(tgt_real * tgt_real + tgt_imag * tgt_imag + EPS_MAG)
        usable_count = lengths * (HOP // stride)
        frame_index = start_sample // stride + jnp.arange(frame_count, dtype=jnp.int32)
        usable = frame_index[None, :, None] < usable_count[:, None, None]
        mag_gap = est_mag - tgt_mag
        log_gap = jnp.log(est_mag) - jnp.log(tgt_mag)
        entries = (usable_count * halfway).astype(jnp.float32)
        spread_list.append(jnp.sum(jnp.where(usable, mag_gap * mag_gap, 0.0), axis=(1, 2)))
        energy_list.append(jnp.sum(jnp.where(usable, tgt_mag * tgt_mag, 0.0), axis=(1, 2)))
        logterm_list.append(
            jnp.sum(jnp.where(usable, log_gap * log_gap, 0.0), axis=(1, 2)) / entries
        )
        saved.append((est_real, est_imag, est_mag, mag_gap, log_gap, usable, entries, table))
    spreads = jnp.stack(spread_list)
    energies = jnp.stack(energy_list)
    logterms = jnp.stack(logterm_list)
    spreads, energies, logterms = lax.psum((spreads, energies, logterms), "seg")
    own_loss = jnp.sum(jnp.sqrt((spreads + EPS_RATIO) / energies) + logterms)
    loss = gathered_sum(own_loss, "clip") / (3 * clip_count * lax.axis_size("clip"))
    ratio_weight = 1.0 / jnp.sqrt((spreads + EPS_RATIO) * energies)
    gradient = jnp.zeros((clip_count, samples), jnp.float32)
    extras = []
    for level, points in enumerate(sizes_list):
        stride = points // 4
        frame_count = samples // stride
        est_real, est_imag, est_mag, mag_gap, log_gap, usable, entries, table = saved[level]
        grad_mag = jnp.where(
            usable,
            mag_gap * ratio_weight[level][:, None, None]
            + 2.0 * log_gap / (est_mag * entries[:, None, None]),
            0.0,
        ) * (frames_all * BINS)
        grad_x = jnp.concatenate(
            [grad_mag * est_real / est_mag, grad_mag * est_imag / est_mag], axis=2
        ).astype(jnp.bfloat16)
        grad_frames = jnp.einsum(
            "cfj,jm->cfm", grad_x, table, preferred_element_type=jnp.float32
        )
        spread_back = spread_parts(grad_frames.reshape(clip_count, frame_count, 4, stride))
        gradient = gradient + spread_back[:, :frame_count].reshape(clip_count, samples)
        extras.append(spread_back[:, frame_count:].reshape(clip_count, 3 * stride))
    halo = 3 * NFFT // 4
    spill = sum(jnp.pad(extra, ((0, 0), (0, halo - extra.shape[1]))) for extra in extras)
    received = shifted(spill, "seg", 1)
    gradient = gradient + jnp.pad(received, ((0, 0), (0, samples - halo)))
    grad_wave = jnp.where(inside, gradient, 0.0).astype(jnp.bfloat16)
    grad_hops = grad_wave.reshape(clip_count, rows_here, HOP)
    portion = lax.all_gather(grad_hops, "seg", axis=1, tiled=True)
    padded = jnp.concatenate([portion, jnp.zeros((clip_count, 3, HOP), portion.dtype)], axis=1)
    grad_signals = jnp.concatenate(
        [padded[:, quarter : quarter + frames_all] for quarter in range(4)], axis=2
    )
    spec_grad = jnp.einsum(
        "ctm,rbm->crbt", grad_signals, local_table, preferred_element_type=jnp.float32
    ).astype(jnp.bfloat16)
    return (loss, spec_grad)


def solution(mesh):
    return jax.shard_map(
        body,
        mesh=mesh,
        in_specs=(P("clip", None, "seg", None), P("clip", "seg"), P("clip")),
        out_specs=(P(), P("clip", None, "seg", None)),
        check_vma=False,
    )
```

```python
import math

import jax
import jax.numpy as jnp
from jax import lax
from jax.sharding import PartitionSpec as P

BINS = 1024
NFFT = 2048
HOP = 512


EPS_MAG = 0.1
EPS_RATIO = 1e-05


def shifted(block, axis, distance):
    devices = range(lax.axis_size(axis))
    route = [(i - distance, i) for i in devices if i - distance in devices]
    return lax.ppermute(block, axis, route)


def angle_pair(index, points):
    angles = (index % points).astype(jnp.float32) * (2.0 * math.pi / points)
    return jnp.cos(angles), jnp.sin(angles)


def window_of(time_index, points):
    return 0.5 - 0.5 * jnp.cos(time_index.astype(jnp.float32) * (2.0 * math.pi / points))


def analysis_table(points):
    halfway = points // 2
    lanes = min(128, halfway)
    groups = halfway // lanes
    time_index = jnp.arange(points, dtype=jnp.int32)[None, :]
    fine = angle_pair(jnp.arange(lanes, dtype=jnp.int32)[:, None] * time_index, points)
    row = jnp.arange(2 * groups, dtype=jnp.int32)[:, None]
    is_sine = row >= groups
    coarse_cos, coarse_sin = angle_pair(((row % groups) * lanes) * time_index, points)
    first = jnp.where(is_sine, -coarse_sin, coarse_cos)
    second = jnp.where(is_sine, -coarse_cos, -coarse_sin)
    scale = window_of(time_index, points) * (1.0 / math.sqrt(points))
    fine_cos, fine_sin = (part * scale for part in fine)
    entry_value = first[:, None, :] * fine_cos[None, :, :] + second[:, None, :] * fine_sin[None, :, :]
    table = entry_value.astype(jnp.bfloat16)
    return lax.optimization_barrier(table.reshape(points, points))


def synthesis_rows(first_bin, band_count):
    sub = 16 if band_count % 16 == 0 else 1
    time_index = jnp.arange(NFFT, dtype=jnp.int32)[None, :]
    row = jnp.arange(2 * (band_count // sub), dtype=jnp.int32)[:, None]
    is_sine = row >= band_count // sub
    coarse_bins = first_bin + sub * (row % (band_count // sub))
    coarse_cos, coarse_sin = angle_pair(coarse_bins * time_index, NFFT)
    scale = window_of(time_index, NFFT) * (1.0 / math.sqrt(BINS))
    fine_cos, fine_sin = (
        part * scale
        for part in angle_pair(jnp.arange(sub, dtype=jnp.int32)[:, None] * time_index, NFFT)
    )
    first = jnp.where(is_sine, -coarse_sin, coarse_cos)
    second = jnp.where(is_sine, -coarse_cos, -coarse_sin)
    entry_value = first[:, None, :] * fine_cos[None, :, :] + second[:, None, :] * fine_sin[None, :, :]
    table = entry_value.astype(jnp.bfloat16)
    return lax.optimization_barrier(table.reshape(2, band_count, NFFT))


def gathered_sum(value, axis):
    size = lax.axis_size(axis)
    here = lax.axis_index(axis)
    held = value[None]
    while held.shape[0] < size and size % (2 * held.shape[0]) == 0:
        distance = held.shape[0]
        route = [(i, (i + distance) % size) for i in range(size)]
        held = jnp.concatenate([held, lax.ppermute(held, axis, route)], axis=0)
    for distance in range(held.shape[0], size):
        route = [(i, (i + distance) % size) for i in range(size)]
        held = jnp.concatenate([held, lax.ppermute(value, axis, route)[None]], axis=0)
    source = (here - jnp.arange(size, dtype=jnp.int32)) % size
    slots = jnp.sum(
        jnp.where(
            (source[:, None] == jnp.arange(size, dtype=jnp.int32)[None, :]).reshape(
                (size, size) + (1,) * value.ndim
            ),
            held[:, None],
            0.0,
        ),
        axis=0,
    )
    return jnp.sum(slots, axis=0)


def spread_parts(quarters):
    return sum(
        (
            jnp.pad(quarters[:, :, quarter], ((0, 0), (quarter, 3 - quarter), (0, 0)))
            for quarter in range(4)
        )
    )


def framed(signal, beyond, stride):
    frame_count = signal.shape[1] // stride
    padded = jnp.concatenate([signal, beyond], axis=1).reshape(
        signal.shape[0], frame_count + 3, stride
    )
    return jnp.concatenate(
        [padded[:, quarter : quarter + frame_count] for quarter in range(4)], axis=2
    )


def body(spectra, target, lengths):
    clip_count = spectra.shape[0]
    band_count = spectra.shape[2]
    frames_all = spectra.shape[3]
    samples = target.shape[1]
    rows_here = samples // HOP
    seg_index = lax.axis_index("seg")
    start_sample = seg_index * samples
    local_table = synthesis_rows(seg_index * band_count, band_count)
    sample_index = start_sample + jnp.arange(samples, dtype=jnp.int32)
    inside = sample_index[None, :] < (lengths * HOP)[:, None]
    clean = jnp.where(inside, target, jnp.zeros_like(target))
    clean, local_table = lax.optimization_barrier((clean, local_table))
    padded_spec = jnp.pad(spectra, ((0, 0), (0, 0), (0, 0), (3, 0)))
    framed_sig = jnp.einsum(
        "crbf,rbm->fcm", padded_spec, local_table, preferred_element_type=jnp.float32
    )
    hop_rows = lax.psum_scatter(
        sum(
            (
                framed_sig[
                    3 - quarter : 3 - quarter + rows_here * lax.axis_size("seg"),
                    :,
                    quarter * HOP : (quarter + 1) * HOP,
                ]
                for quarter in range(4)
            )
        ),
        "seg",
        scatter_dimension=0,
        tiled=True,
    )
    estimate = jnp.transpose(hop_rows, (1, 0, 2)).reshape(clip_count, samples)
    est_wave = jnp.where(inside, estimate, 0.0).astype(jnp.bfloat16)
    sizes_list = (NFFT // 4, NFFT // 2, NFFT)
    halo = 3 * NFFT // 4
    clean_beyond = shifted(clean[:, :halo], "seg", -1)
    est_beyond = shifted(est_wave[:, :halo], "seg", -1)
    saved = []
    spread_list = []
    energy_list = []
    logterm_list = []
    for points in sizes_list:
        stride = points // 4
        halfway = points // 2
        frame_count = samples // stride
        table = analysis_table(points)
        tgt_x = jnp.einsum(
            "cfm,jm->cfj",
            framed(clean, clean_beyond[:, : 3 * stride], stride),
            table,
            preferred_element_type=jnp.float32,
        )
        est_x = jnp.einsum(
            "cfm,jm->cfj",
            framed(est_wave, est_beyond[:, : 3 * stride], stride),
            table,
            preferred_element_type=jnp.float32,
        )
        est_real = est_x[:, :, :halfway]
        est_imag = est_x[:, :, halfway:]
        tgt_real = tgt_x[:, :, :halfway]
        tgt_imag = tgt_x[:, :, halfway:]
        est_mag = jnp.sqrt(est_real * est_real + est_imag * est_imag + EPS_MAG)
        tgt_mag = jnp.sqrt(tgt_real * tgt_real + tgt_imag * tgt_imag + EPS_MAG)
        usable_count = lengths * (HOP // stride)
        frame_index = start_sample // stride + jnp.arange(frame_count, dtype=jnp.int32)
        usable = frame_index[None, :, None] < usable_count[:, None, None]
        mag_gap = est_mag - tgt_mag
        log_gap = jnp.log(est_mag) - jnp.log(tgt_mag)
        entries = (usable_count * halfway).astype(jnp.float32)
        spread_list.append(jnp.sum(jnp.where(usable, mag_gap * mag_gap, 0.0), axis=(1, 2)))
        energy_list.append(jnp.sum(jnp.where(usable, tgt_mag * tgt_mag, 0.0), axis=(1, 2)))
        logterm_list.append(
            jnp.sum(jnp.where(usable, log_gap * log_gap, 0.0), axis=(1, 2)) / entries
        )
        saved.append((est_real, est_imag, est_mag, mag_gap, log_gap, usable, entries, table))
    spreads = jnp.stack(spread_list)
    energies = jnp.stack(energy_list)
    logterms = jnp.stack(logterm_list)
    parts = lax.all_gather(jnp.stack([spreads, energies, logterms]), "seg", axis=0, tiled=False)
    spreads, energies, logterms = jnp.sum(parts, axis=0)
    own_loss = jnp.sum(jnp.sqrt((spreads + EPS_RATIO) / energies) + logterms)
    loss = gathered_sum(own_loss, "clip") / (3 * clip_count * lax.axis_size("clip"))
    ratio_weight = 1.0 / jnp.sqrt((spreads + EPS_RATIO) * energies)
    gradient = jnp.zeros((clip_count, samples), jnp.float32)
    extras = []
    for level, points in enumerate(sizes_list):
        stride = points // 4
        frame_count = samples // stride
        est_real, est_imag, est_mag, mag_gap, log_gap, usable, entries, table = saved[level]
        grad_mag = jnp.where(
            usable,
            mag_gap * ratio_weight[level][:, None, None]
            + 2.0 * log_gap / (est_mag * entries[:, None, None]),
            0.0,
        ) * (frames_all * BINS)
        grad_x = jnp.concatenate(
            [grad_mag * est_real / est_mag, grad_mag * est_imag / est_mag], axis=2
        ).astype(jnp.bfloat16)
        grad_frames = jnp.einsum(
            "cfj,jm->cfm", grad_x, table, preferred_element_type=jnp.float32
        )
        spread_back = spread_parts(grad_frames.reshape(clip_count, frame_count, 4, stride))
        gradient = gradient + spread_back[:, :frame_count].reshape(clip_count, samples)
        extras.append(spread_back[:, frame_count:].reshape(clip_count, 3 * stride))
    halo = 3 * NFFT // 4
    spill = sum(jnp.pad(extra, ((0, 0), (0, halo - extra.shape[1]))) for extra in extras)
    received = shifted(spill, "seg", 1)
    gradient = gradient + jnp.pad(received, ((0, 0), (0, samples - halo)))
    grad_wave = jnp.where(inside, gradient, 0.0).astype(jnp.bfloat16)
    grad_hops = grad_wave.reshape(clip_count, rows_here, HOP)
    portion = lax.all_gather(grad_hops, "seg", axis=1, tiled=True)
    padded = jnp.concatenate([portion, jnp.zeros((clip_count, 3, HOP), portion.dtype)], axis=1)
    grad_signals = jnp.concatenate(
        [padded[:, quarter : quarter + frames_all] for quarter in range(4)], axis=2
    )
    spec_grad = jnp.einsum(
        "ctm,rbm->crbt", grad_signals, local_table, preferred_element_type=jnp.float32
    ).astype(jnp.bfloat16)
    return (loss, spec_grad)


def solution(mesh):
    return jax.shard_map(
        body,
        mesh=mesh,
        in_specs=(P("clip", None, "seg", None), P("clip", "seg"), P("clip")),
        out_specs=(P(), P("clip", None, "seg", None)),
        check_vma=False,
    )
```

```python
import math

import jax
import jax.numpy as jnp
from jax import lax
from jax.sharding import PartitionSpec as P

BINS = 1024
NFFT = 2048
HOP = 512


EPS_MAG = 0.1
EPS_RATIO = 1e-05


def shifted(block, axis, distance):
    devices = range(lax.axis_size(axis))
    route = [(i - distance, i) for i in devices if i - distance in devices]
    return lax.ppermute(block, axis, route)


def angle_pair(index, points):
    angles = (index % points).astype(jnp.float32) * (2.0 * math.pi / points)
    return jnp.cos(angles), jnp.sin(angles)


def window_of(time_index, points):
    return 0.5 - 0.5 * jnp.cos(time_index.astype(jnp.float32) * (2.0 * math.pi / points))


def analysis_table(points):
    halfway = points // 2
    lanes = min(128, halfway)
    groups = halfway // lanes
    time_index = jnp.arange(points, dtype=jnp.int32)[None, :]
    fine = angle_pair(jnp.arange(lanes, dtype=jnp.int32)[:, None] * time_index, points)
    row = jnp.arange(2 * groups, dtype=jnp.int32)[:, None]
    is_sine = row >= groups
    coarse_cos, coarse_sin = angle_pair(((row % groups) * lanes) * time_index, points)
    first = jnp.where(is_sine, -coarse_sin, coarse_cos)
    second = jnp.where(is_sine, -coarse_cos, -coarse_sin)
    scale = window_of(time_index, points) * (1.0 / math.sqrt(points))
    fine_cos, fine_sin = (part * scale for part in fine)
    entry_value = first[:, None, :] * fine_cos[None, :, :] + second[:, None, :] * fine_sin[None, :, :]
    table = entry_value.astype(jnp.bfloat16)
    return lax.optimization_barrier(table.reshape(points, points))


def synthesis_rows(first_bin, band_count):
    sub = 16 if band_count % 16 == 0 else 1
    time_index = jnp.arange(NFFT, dtype=jnp.int32)[None, :]
    row = jnp.arange(2 * (band_count // sub), dtype=jnp.int32)[:, None]
    is_sine = row >= band_count // sub
    coarse_bins = first_bin + sub * (row % (band_count // sub))
    coarse_cos, coarse_sin = angle_pair(coarse_bins * time_index, NFFT)
    scale = window_of(time_index, NFFT) * (1.0 / math.sqrt(BINS))
    fine_cos, fine_sin = (
        part * scale
        for part in angle_pair(jnp.arange(sub, dtype=jnp.int32)[:, None] * time_index, NFFT)
    )
    first = jnp.where(is_sine, -coarse_sin, coarse_cos)
    second = jnp.where(is_sine, -coarse_cos, -coarse_sin)
    entry_value = first[:, None, :] * fine_cos[None, :, :] + second[:, None, :] * fine_sin[None, :, :]
    table = entry_value.astype(jnp.bfloat16)
    return lax.optimization_barrier(table.reshape(2, band_count, NFFT))


def ring_gathered(value, axis):
    size = lax.axis_size(axis)
    here = lax.axis_index(axis)
    held = [value]
    for distance in range(1, size):
        route = [(i, (i + distance) % size) for i in range(size)]
        held.append(lax.ppermute(value, axis, route))
    held = jnp.stack(held)
    source = (here - jnp.arange(size, dtype=jnp.int32)) % size
    pick = source[:, None] == jnp.arange(size, dtype=jnp.int32)[None, :]
    return jnp.sum(
        jnp.where(pick.reshape((size, size) + (1,) * value.ndim), held[:, None], 0.0), axis=0
    )


def spread_parts(quarters):
    return sum(
        (
            jnp.pad(quarters[:, :, quarter], ((0, 0), (quarter, 3 - quarter), (0, 0)))
            for quarter in range(4)
        )
    )


def framed(signal, beyond, stride):
    frame_count = signal.shape[1] // stride
    padded = jnp.concatenate([signal, beyond], axis=1).reshape(
        signal.shape[0], frame_count + 3, stride
    )
    return jnp.concatenate(
        [padded[:, quarter : quarter + frame_count] for quarter in range(4)], axis=2
    )


def body(spectra, target, lengths):
    clip_count = spectra.shape[0]
    band_count = spectra.shape[2]
    frames_all = spectra.shape[3]
    samples = target.shape[1]
    rows_here = samples // HOP
    seg_index = lax.axis_index("seg")
    start_sample = seg_index * samples
    local_table = synthesis_rows(seg_index * band_count, band_count)
    sample_index = start_sample + jnp.arange(samples, dtype=jnp.int32)
    inside = sample_index[None, :] < (lengths * HOP)[:, None]
    clean = jnp.where(inside, target, jnp.zeros_like(target))
    clean, local_table = lax.optimization_barrier((clean, local_table))
    padded_spec = jnp.pad(spectra, ((0, 0), (0, 0), (0, 0), (3, 0)))
    framed_sig = jnp.einsum(
        "crbf,rbm->fcm", padded_spec, local_table, preferred_element_type=jnp.float32
    )
    hop_rows = lax.psum_scatter(
        sum(
            (
                framed_sig[
                    3 - quarter : 3 - quarter + rows_here * lax.axis_size("seg"),
                    :,
                    quarter * HOP : (quarter + 1) * HOP,
                ]
                for quarter in range(4)
            )
        ),
        "seg",
        scatter_dimension=0,
        tiled=True,
    )
    estimate = jnp.transpose(hop_rows, (1, 0, 2)).reshape(clip_count, samples)
    est_wave = jnp.where(inside, estimate, 0.0).astype(jnp.bfloat16)
    sizes_list = (NFFT // 4, NFFT // 2, NFFT)
    halo = 3 * NFFT // 4
    clean_beyond = shifted(clean[:, :halo], "seg", -1)
    est_beyond = shifted(est_wave[:, :halo], "seg", -1)
    saved = []
    spread_list = []
    energy_list = []
    logterm_list = []
    for points in sizes_list:
        stride = points // 4
        halfway = points // 2
        frame_count = samples // stride
        table = analysis_table(points)
        tgt_x = jnp.einsum(
            "cfm,jm->cfj",
            framed(clean, clean_beyond[:, : 3 * stride], stride),
            table,
            preferred_element_type=jnp.float32,
        )
        est_x = jnp.einsum(
            "cfm,jm->cfj",
            framed(est_wave, est_beyond[:, : 3 * stride], stride),
            table,
            preferred_element_type=jnp.float32,
        )
        est_real = est_x[:, :, :halfway]
        est_imag = est_x[:, :, halfway:]
        tgt_real = tgt_x[:, :, :halfway]
        tgt_imag = tgt_x[:, :, halfway:]
        est_mag = jnp.sqrt(est_real * est_real + est_imag * est_imag + EPS_MAG)
        tgt_mag = jnp.sqrt(tgt_real * tgt_real + tgt_imag * tgt_imag + EPS_MAG)
        usable_count = lengths * (HOP // stride)
        frame_index = start_sample // stride + jnp.arange(frame_count, dtype=jnp.int32)
        usable = frame_index[None, :, None] < usable_count[:, None, None]
        mag_gap = est_mag - tgt_mag
        log_gap = jnp.log(est_mag) - jnp.log(tgt_mag)
        entries = (usable_count * halfway).astype(jnp.float32)
        spread_list.append(jnp.sum(jnp.where(usable, mag_gap * mag_gap, 0.0), axis=(1, 2)))
        energy_list.append(jnp.sum(jnp.where(usable, tgt_mag * tgt_mag, 0.0), axis=(1, 2)))
        logterm_list.append(
            jnp.sum(jnp.where(usable, log_gap * log_gap, 0.0), axis=(1, 2)) / entries
        )
        saved.append((est_real, est_imag, est_mag, mag_gap, log_gap, usable, entries, table))
    spreads = jnp.stack(spread_list)
    energies = jnp.stack(energy_list)
    logterms = jnp.stack(logterm_list)
    groups = ring_gathered(jnp.stack([spreads, energies, logterms]), "clip")
    totals = jnp.sum(lax.all_gather(groups, "seg", axis=0, tiled=False), axis=0)
    loss = jnp.sum(jnp.sqrt((totals[:, 0] + EPS_RATIO) / totals[:, 1]) + totals[:, 2]) / (
        3 * clip_count * lax.axis_size("clip")
    )
    spreads, energies, logterms = totals[lax.axis_index("clip")]
    ratio_weight = 1.0 / jnp.sqrt((spreads + EPS_RATIO) * energies)
    gradient = jnp.zeros((clip_count, samples), jnp.float32)
    extras = []
    for level, points in enumerate(sizes_list):
        stride = points // 4
        frame_count = samples // stride
        est_real, est_imag, est_mag, mag_gap, log_gap, usable, entries, table = saved[level]
        grad_mag = jnp.where(
            usable,
            mag_gap * ratio_weight[level][:, None, None]
            + 2.0 * log_gap / (est_mag * entries[:, None, None]),
            0.0,
        ) * (frames_all * BINS)
        grad_x = jnp.concatenate(
            [grad_mag * est_real / est_mag, grad_mag * est_imag / est_mag], axis=2
        ).astype(jnp.bfloat16)
        grad_frames = jnp.einsum(
            "cfj,jm->cfm", grad_x, table, preferred_element_type=jnp.float32
        )
        spread_back = spread_parts(grad_frames.reshape(clip_count, frame_count, 4, stride))
        gradient = gradient + spread_back[:, :frame_count].reshape(clip_count, samples)
        extras.append(spread_back[:, frame_count:].reshape(clip_count, 3 * stride))
    halo = 3 * NFFT // 4
    spill = sum(jnp.pad(extra, ((0, 0), (0, halo - extra.shape[1]))) for extra in extras)
    received = shifted(spill, "seg", 1)
    gradient = gradient + jnp.pad(received, ((0, 0), (0, samples - halo)))
    grad_wave = jnp.where(inside, gradient, 0.0).astype(jnp.bfloat16)
    grad_hops = grad_wave.reshape(clip_count, rows_here, HOP)
    portion = lax.all_gather(grad_hops, "seg", axis=1, tiled=True)
    padded = jnp.concatenate([portion, jnp.zeros((clip_count, 3, HOP), portion.dtype)], axis=1)
    grad_signals = jnp.concatenate(
        [padded[:, quarter : quarter + frames_all] for quarter in range(4)], axis=2
    )
    spec_grad = jnp.einsum(
        "ctm,rbm->crbt", grad_signals, local_table, preferred_element_type=jnp.float32
    ).astype(jnp.bfloat16)
    return (loss, spec_grad)


def solution(mesh):
    return jax.shard_map(
        body,
        mesh=mesh,
        in_specs=(P("clip", None, "seg", None), P("clip", "seg"), P("clip")),
        out_specs=(P(), P("clip", None, "seg", None)),
        check_vma=False,
    )
```

```python
import math

import jax
import jax.numpy as jnp
from jax import lax
from jax.sharding import PartitionSpec as P

BINS = 1024
NFFT = 2048
HOP = 512


EPS_MAG = 0.1
EPS_RATIO = 1e-05


def shifted(block, axis, distance):
    devices = range(lax.axis_size(axis))
    route = [(i - distance, i) for i in devices if i - distance in devices]
    return lax.ppermute(block, axis, route)


def angle_pair(index, points):
    angles = (index % points).astype(jnp.float32) * (2.0 * math.pi / points)
    return jnp.cos(angles), jnp.sin(angles)


def window_of(time_index, points):
    return 0.5 - 0.5 * jnp.cos(time_index.astype(jnp.float32) * (2.0 * math.pi / points))


def analysis_table(points):
    halfway = points // 2
    lanes = min(128, halfway)
    groups = halfway // lanes
    time_index = jnp.arange(points, dtype=jnp.int32)[None, :]
    fine = angle_pair(jnp.arange(lanes, dtype=jnp.int32)[:, None] * time_index, points)
    row = jnp.arange(2 * groups, dtype=jnp.int32)[:, None]
    is_sine = row >= groups
    coarse_cos, coarse_sin = angle_pair(((row % groups) * lanes) * time_index, points)
    first = jnp.where(is_sine, -coarse_sin, coarse_cos)
    second = jnp.where(is_sine, -coarse_cos, -coarse_sin)
    scale = window_of(time_index, points) * (1.0 / math.sqrt(points))
    fine_cos, fine_sin = (part * scale for part in fine)
    entry_value = first[:, None, :] * fine_cos[None, :, :] + second[:, None, :] * fine_sin[None, :, :]
    table = entry_value.astype(jnp.bfloat16)
    return lax.optimization_barrier(table.reshape(points, points))


def synthesis_rows(first_bin, band_count):
    sub = 16 if band_count % 16 == 0 else 1
    time_index = jnp.arange(NFFT, dtype=jnp.int32)[None, :]
    row = jnp.arange(2 * (band_count // sub), dtype=jnp.int32)[:, None]
    is_sine = row >= band_count // sub
    coarse_bins = first_bin + sub * (row % (band_count // sub))
    coarse_cos, coarse_sin = angle_pair(coarse_bins * time_index, NFFT)
    scale = window_of(time_index, NFFT) * (1.0 / math.sqrt(BINS))
    fine_cos, fine_sin = (
        part * scale
        for part in angle_pair(jnp.arange(sub, dtype=jnp.int32)[:, None] * time_index, NFFT)
    )
    first = jnp.where(is_sine, -coarse_sin, coarse_cos)
    second = jnp.where(is_sine, -coarse_cos, -coarse_sin)
    entry_value = first[:, None, :] * fine_cos[None, :, :] + second[:, None, :] * fine_sin[None, :, :]
    table = entry_value.astype(jnp.bfloat16)
    return lax.optimization_barrier(table.reshape(2, band_count, NFFT))


def gathered_sum(value, axis):
    size = lax.axis_size(axis)
    here = lax.axis_index(axis)
    held = value[None]
    while held.shape[0] < size and size % (2 * held.shape[0]) == 0:
        distance = held.shape[0]
        route = [(i, (i + distance) % size) for i in range(size)]
        held = jnp.concatenate([held, lax.ppermute(held, axis, route)], axis=0)
    for distance in range(held.shape[0], size):
        route = [(i, (i + distance) % size) for i in range(size)]
        held = jnp.concatenate([held, lax.ppermute(value, axis, route)[None]], axis=0)
    source = (here - jnp.arange(size, dtype=jnp.int32)) % size
    slots = jnp.sum(
        jnp.where(
            (source[:, None] == jnp.arange(size, dtype=jnp.int32)[None, :]).reshape(
                (size, size) + (1,) * value.ndim
            ),
            held[:, None],
            0.0,
        ),
        axis=0,
    )
    return jnp.sum(slots, axis=0)


def spread_parts(quarters):
    return sum(
        (
            jnp.pad(quarters[:, :, quarter], ((0, 0), (quarter, 3 - quarter), (0, 0)))
            for quarter in range(4)
        )
    )


def framed(signal, beyond, stride):
    frame_count = signal.shape[1] // stride
    padded = jnp.concatenate([signal, beyond], axis=1).reshape(
        signal.shape[0], frame_count + 3, stride
    )
    return jnp.concatenate(
        [padded[:, quarter : quarter + frame_count] for quarter in range(4)], axis=2
    )


def body(spectra, target, lengths):
    clip_count = spectra.shape[0]
    band_count = spectra.shape[2]
    frames_all = spectra.shape[3]
    samples = target.shape[1]
    rows_here = samples // HOP
    seg_index = lax.axis_index("seg")
    start_sample = seg_index * samples
    local_table = synthesis_rows(seg_index * band_count, band_count)
    sample_index = start_sample + jnp.arange(samples, dtype=jnp.int32)
    inside = sample_index[None, :] < (lengths * HOP)[:, None]
    clean = jnp.where(inside, target, jnp.zeros_like(target))
    clean, local_table = lax.optimization_barrier((clean, local_table))
    padded_spec = jnp.pad(spectra, ((0, 0), (0, 0), (0, 0), (3, 0)))
    hop_count = rows_here * lax.axis_size("seg")
    shifted_spec = jnp.stack(
        [padded_spec[:, :, :, 3 - quarter : 3 - quarter + hop_count] for quarter in range(4)],
        axis=1,
    )
    quarter_table = local_table.reshape(2, band_count, 4, HOP)
    hop_rows = lax.psum_scatter(
        jnp.einsum(
            "cqrbh,rbqi->hci", shifted_spec, quarter_table, preferred_element_type=jnp.float32
        ),
        "seg",
        scatter_dimension=0,
        tiled=True,
    )
    estimate = jnp.transpose(hop_rows, (1, 0, 2)).reshape(clip_count, samples)
    est_wave = jnp.where(inside, estimate, 0.0).astype(jnp.bfloat16)
    sizes_list = (NFFT // 4, NFFT // 2, NFFT)
    halo = 3 * NFFT // 4
    clean_beyond = shifted(clean[:, :halo], "seg", -1)
    est_beyond = shifted(est_wave[:, :halo], "seg", -1)
    saved = []
    spread_list = []
    energy_list = []
    logterm_list = []
    for points in sizes_list:
        stride = points // 4
        halfway = points // 2
        frame_count = samples // stride
        table = analysis_table(points)
        tgt_x = jnp.einsum(
            "cfm,jm->cfj",
            framed(clean, clean_beyond[:, : 3 * stride], stride),
            table,
            preferred_element_type=jnp.float32,
        )
        est_x = jnp.einsum(
            "cfm,jm->cfj",
            framed(est_wave, est_beyond[:, : 3 * stride], stride),
            table,
            preferred_element_type=jnp.float32,
        )
        est_real = est_x[:, :, :halfway]
        est_imag = est_x[:, :, halfway:]
        tgt_real = tgt_x[:, :, :halfway]
        tgt_imag = tgt_x[:, :, halfway:]
        est_mag = jnp.sqrt(est_real * est_real + est_imag * est_imag + EPS_MAG)
        tgt_mag = jnp.sqrt(tgt_real * tgt_real + tgt_imag * tgt_imag + EPS_MAG)
        usable_count = lengths * (HOP // stride)
        frame_index = start_sample // stride + jnp.arange(frame_count, dtype=jnp.int32)
        usable = frame_index[None, :, None] < usable_count[:, None, None]
        mag_gap = est_mag - tgt_mag
        log_gap = jnp.log(est_mag) - jnp.log(tgt_mag)
        entries = (usable_count * halfway).astype(jnp.float32)
        spread_list.append(jnp.sum(jnp.where(usable, mag_gap * mag_gap, 0.0), axis=(1, 2)))
        energy_list.append(jnp.sum(jnp.where(usable, tgt_mag * tgt_mag, 0.0), axis=(1, 2)))
        logterm_list.append(
            jnp.sum(jnp.where(usable, log_gap * log_gap, 0.0), axis=(1, 2)) / entries
        )
        saved.append((est_real, est_imag, est_mag, mag_gap, log_gap, usable, entries, table))
    spreads = jnp.stack(spread_list)
    energies = jnp.stack(energy_list)
    logterms = jnp.stack(logterm_list)
    parts = lax.all_gather(jnp.stack([spreads, energies, logterms]), "seg", axis=0, tiled=False)
    spreads, energies, logterms = jnp.sum(parts, axis=0)
    own_loss = jnp.sum(jnp.sqrt((spreads + EPS_RATIO) / energies) + logterms)
    loss = gathered_sum(own_loss, "clip") / (3 * clip_count * lax.axis_size("clip"))
    ratio_weight = 1.0 / jnp.sqrt((spreads + EPS_RATIO) * energies)
    gradient = jnp.zeros((clip_count, samples), jnp.float32)
    extras = []
    for level, points in enumerate(sizes_list):
        stride = points // 4
        frame_count = samples // stride
        est_real, est_imag, est_mag, mag_gap, log_gap, usable, entries, table = saved[level]
        grad_mag = jnp.where(
            usable,
            mag_gap * ratio_weight[level][:, None, None]
            + 2.0 * log_gap / (est_mag * entries[:, None, None]),
            0.0,
        ) * (frames_all * BINS)
        grad_x = jnp.concatenate(
            [grad_mag * est_real / est_mag, grad_mag * est_imag / est_mag], axis=2
        ).astype(jnp.bfloat16)
        grad_frames = jnp.einsum(
            "cfj,jm->cfm", grad_x, table, preferred_element_type=jnp.float32
        )
        spread_back = spread_parts(grad_frames.reshape(clip_count, frame_count, 4, stride))
        gradient = gradient + spread_back[:, :frame_count].reshape(clip_count, samples)
        extras.append(spread_back[:, frame_count:].reshape(clip_count, 3 * stride))
    halo = 3 * NFFT // 4
    spill = sum(jnp.pad(extra, ((0, 0), (0, halo - extra.shape[1]))) for extra in extras)
    received = shifted(spill, "seg", 1)
    gradient = gradient + jnp.pad(received, ((0, 0), (0, samples - halo)))
    grad_wave = jnp.where(inside, gradient, 0.0).astype(jnp.bfloat16)
    grad_hops = grad_wave.reshape(clip_count, rows_here, HOP)
    portion = lax.all_gather(grad_hops, "seg", axis=1, tiled=True)
    padded = jnp.concatenate([portion, jnp.zeros((clip_count, 3, HOP), portion.dtype)], axis=1)
    grad_signals = jnp.concatenate(
        [padded[:, quarter : quarter + frames_all] for quarter in range(4)], axis=2
    )
    spec_grad = jnp.einsum(
        "ctm,rbm->crbt", grad_signals, local_table, preferred_element_type=jnp.float32
    ).astype(jnp.bfloat16)
    return (loss, spec_grad)


def solution(mesh):
    return jax.shard_map(
        body,
        mesh=mesh,
        in_specs=(P("clip", None, "seg", None), P("clip", "seg"), P("clip")),
        out_specs=(P(), P("clip", None, "seg", None)),
        check_vma=False,
    )
```

```python
import math

import jax
import jax.numpy as jnp
from jax import lax
from jax.sharding import PartitionSpec as P

BINS = 1024
NFFT = 2048
HOP = 512


EPS_MAG = 0.1
EPS_RATIO = 1e-05


def shifted(block, axis, distance):
    devices = range(lax.axis_size(axis))
    route = [(i - distance, i) for i in devices if i - distance in devices]
    return lax.ppermute(block, axis, route)


def angle_pair(index, points):
    angles = (index % points).astype(jnp.float32) * (2.0 * math.pi / points)
    return jnp.cos(angles), jnp.sin(angles)


def window_of(time_index, points):
    return 0.5 - 0.5 * jnp.cos(time_index.astype(jnp.float32) * (2.0 * math.pi / points))


def analysis_table(points):
    halfway = points // 2
    lanes = min(128, halfway)
    groups = halfway // lanes
    time_index = jnp.arange(points, dtype=jnp.int32)[None, :]
    fine = angle_pair(jnp.arange(lanes, dtype=jnp.int32)[:, None] * time_index, points)
    row = jnp.arange(2 * groups, dtype=jnp.int32)[:, None]
    is_sine = row >= groups
    coarse_cos, coarse_sin = angle_pair(((row % groups) * lanes) * time_index, points)
    first = jnp.where(is_sine, -coarse_sin, coarse_cos)
    second = jnp.where(is_sine, -coarse_cos, -coarse_sin)
    scale = window_of(time_index, points) * (1.0 / math.sqrt(points))
    fine_cos, fine_sin = (part * scale for part in fine)
    entry_value = first[:, None, :] * fine_cos[None, :, :] + second[:, None, :] * fine_sin[None, :, :]
    table = entry_value.astype(jnp.bfloat16)
    return lax.optimization_barrier(table.reshape(points, points))


def synthesis_rows(first_bin, band_count):
    sub = 16 if band_count % 16 == 0 else 1
    time_index = jnp.arange(NFFT, dtype=jnp.int32)[None, :]
    row = jnp.arange(2 * (band_count // sub), dtype=jnp.int32)[:, None]
    is_sine = row >= band_count // sub
    coarse_bins = first_bin + sub * (row % (band_count // sub))
    coarse_cos, coarse_sin = angle_pair(coarse_bins * time_index, NFFT)
    scale = window_of(time_index, NFFT) * (1.0 / math.sqrt(BINS))
    fine_cos, fine_sin = (
        part * scale
        for part in angle_pair(jnp.arange(sub, dtype=jnp.int32)[:, None] * time_index, NFFT)
    )
    first = jnp.where(is_sine, -coarse_sin, coarse_cos)
    second = jnp.where(is_sine, -coarse_cos, -coarse_sin)
    entry_value = first[:, None, :] * fine_cos[None, :, :] + second[:, None, :] * fine_sin[None, :, :]
    table = entry_value.astype(jnp.bfloat16)
    return lax.optimization_barrier(table.reshape(2, band_count, NFFT))


def gathered_sum(value, axis):
    size = lax.axis_size(axis)
    here = lax.axis_index(axis)
    devices = range(size)
    slots = jnp.zeros((size,) + value.shape, value.dtype)
    for distance in range(size):
        if distance == 0:
            arrived = value
        else:
            route = [(i, (i + distance) % size) for i in devices]
            arrived = lax.ppermute(value, axis, route)
        source = (here - distance) % size
        slots = slots + jnp.where(
            (jnp.arange(size, dtype=jnp.int32) == source).reshape((size,) + (1,) * value.ndim),
            arrived[None],
            0.0,
        )
    return jnp.sum(slots, axis=0)


def spread_parts(quarters):
    return sum(
        (
            jnp.pad(quarters[:, :, quarter], ((0, 0), (quarter, 3 - quarter), (0, 0)))
            for quarter in range(4)
        )
    )


def framed(signal, beyond, stride):
    frame_count = signal.shape[1] // stride
    padded = jnp.concatenate([signal, beyond], axis=1).reshape(
        signal.shape[0], frame_count + 3, stride
    )
    return jnp.concatenate(
        [padded[:, quarter : quarter + frame_count] for quarter in range(4)], axis=2
    )


def body(spectra, target, lengths):
    clip_count = spectra.shape[0]
    band_count = spectra.shape[2]
    frames_all = spectra.shape[3]
    samples = target.shape[1]
    rows_here = samples // HOP
    seg_index = lax.axis_index("seg")
    start_sample = seg_index * samples
    local_table = synthesis_rows(seg_index * band_count, band_count)
    sample_index = start_sample + jnp.arange(samples, dtype=jnp.int32)
    inside = sample_index[None, :] < (lengths * HOP)[:, None]
    clean = jnp.where(inside, target, jnp.zeros_like(target))
    clean, local_table = lax.optimization_barrier((clean, local_table))
    padded_spec = jnp.pad(spectra, ((0, 0), (0, 0), (0, 0), (3, 0)))
    framed_sig = jnp.einsum(
        "crbf,rbm->fcm", padded_spec, local_table, preferred_element_type=jnp.float32
    )
    hop_rows = lax.psum_scatter(
        sum(
            (
                framed_sig[
                    3 - quarter : 3 - quarter + rows_here * lax.axis_size("seg"),
                    :,
                    quarter * HOP : (quarter + 1) * HOP,
                ]
                for quarter in range(4)
            )
        ),
        "seg",
        scatter_dimension=0,
        tiled=True,
    )
    estimate = jnp.transpose(hop_rows, (1, 0, 2)).reshape(clip_count, samples)
    est_wave = jnp.where(inside, estimate, 0.0).astype(jnp.bfloat16)
    sizes_list = (NFFT // 4, NFFT // 2, NFFT)
    halo = 3 * NFFT // 4
    clean_beyond = shifted(clean[:, :halo], "seg", -1)
    est_beyond = shifted(est_wave[:, :halo], "seg", -1)
    saved = []
    spread_list = []
    energy_list = []
    logterm_list = []
    for points in sizes_list:
        stride = points // 4
        halfway = points // 2
        frame_count = samples // stride
        table = analysis_table(points)
        tgt_x = jnp.einsum(
            "cfm,jm->cfj",
            framed(clean, clean_beyond[:, : 3 * stride], stride),
            table,
            preferred_element_type=jnp.float32,
        )
        est_x = jnp.einsum(
            "cfm,jm->cfj",
            framed(est_wave, est_beyond[:, : 3 * stride], stride),
            table,
            preferred_element_type=jnp.float32,
        )
        est_real = est_x[:, :, :halfway]
        est_imag = est_x[:, :, halfway:]
        tgt_real = tgt_x[:, :, :halfway]
        tgt_imag = tgt_x[:, :, halfway:]
        est_mag = jnp.sqrt(est_real * est_real + est_imag * est_imag + EPS_MAG)
        tgt_mag = jnp.sqrt(tgt_real * tgt_real + tgt_imag * tgt_imag + EPS_MAG)
        usable_count = lengths * (HOP // stride)
        frame_index = start_sample // stride + jnp.arange(frame_count, dtype=jnp.int32)
        usable = frame_index[None, :, None] < usable_count[:, None, None]
        mag_gap = est_mag - tgt_mag
        log_gap = jnp.log(est_mag) - jnp.log(tgt_mag)
        entries = (usable_count * halfway).astype(jnp.float32)
        spread_list.append(jnp.sum(jnp.where(usable, mag_gap * mag_gap, 0.0), axis=(1, 2)))
        energy_list.append(jnp.sum(jnp.where(usable, tgt_mag * tgt_mag, 0.0), axis=(1, 2)))
        logterm_list.append(
            jnp.sum(jnp.where(usable, log_gap * log_gap, 0.0), axis=(1, 2)) / entries
        )
        saved.append((est_real, est_imag, est_mag, mag_gap, log_gap, usable, entries, table))
    spreads = jnp.stack(spread_list)
    energies = jnp.stack(energy_list)
    logterms = jnp.stack(logterm_list)
    parts = lax.all_gather(jnp.stack([spreads, energies, logterms]), "seg", axis=0, tiled=False)
    spreads, energies, logterms = jnp.sum(parts, axis=0)
    own_loss = jnp.sum(jnp.sqrt((spreads + EPS_RATIO) / energies) + logterms)
    loss = gathered_sum(own_loss, "clip") / (3 * clip_count * lax.axis_size("clip"))
    ratio_weight = 1.0 / jnp.sqrt((spreads + EPS_RATIO) * energies)
    gradient = jnp.zeros((clip_count, samples), jnp.float32)
    extras = []
    for level, points in enumerate(sizes_list):
        stride = points // 4
        frame_count = samples // stride
        est_real, est_imag, est_mag, mag_gap, log_gap, usable, entries, table = saved[level]
        grad_mag = jnp.where(
            usable,
            mag_gap * ratio_weight[level][:, None, None]
            + 2.0 * log_gap / (est_mag * entries[:, None, None]),
            0.0,
        ) * (frames_all * BINS)
        grad_x = jnp.concatenate(
            [grad_mag * est_real / est_mag, grad_mag * est_imag / est_mag], axis=2
        ).astype(jnp.bfloat16)
        grad_frames = jnp.einsum(
            "cfj,jm->cfm", grad_x, table, preferred_element_type=jnp.float32
        )
        spread_back = spread_parts(grad_frames.reshape(clip_count, frame_count, 4, stride))
        gradient = gradient + spread_back[:, :frame_count].reshape(clip_count, samples)
        extras.append(spread_back[:, frame_count:].reshape(clip_count, 3 * stride))
    halo = 3 * NFFT // 4
    spill = sum(jnp.pad(extra, ((0, 0), (0, halo - extra.shape[1]))) for extra in extras)
    received = shifted(spill, "seg", 1)
    gradient = gradient + jnp.pad(received, ((0, 0), (0, samples - halo)))
    grad_wave = jnp.where(inside, gradient, 0.0).astype(jnp.bfloat16)
    grad_hops = grad_wave.reshape(clip_count, rows_here, HOP)
    portion = lax.all_gather(grad_hops, "seg", axis=1, tiled=True)
    padded = jnp.concatenate([portion, jnp.zeros((clip_count, 3, HOP), portion.dtype)], axis=1)
    grad_signals = jnp.concatenate(
        [padded[:, quarter : quarter + frames_all] for quarter in range(4)], axis=2
    )
    spec_grad = jnp.einsum(
        "ctm,rbm->crbt", grad_signals, local_table, preferred_element_type=jnp.float32
    ).astype(jnp.bfloat16)
    return (loss, spec_grad)


def solution(mesh):
    return jax.shard_map(
        body,
        mesh=mesh,
        in_specs=(P("clip", None, "seg", None), P("clip", "seg"), P("clip")),
        out_specs=(P(), P("clip", None, "seg", None)),
        check_vma=False,
    )
```

```python
import math

import jax
import jax.numpy as jnp
from jax import lax
from jax.sharding import PartitionSpec as P

BINS = 1024
NFFT = 2048
HOP = 512


EPS_MAG = 0.1
EPS_RATIO = 1e-05


def shifted(block, axis, distance):
    devices = range(lax.axis_size(axis))
    route = [(i - distance, i) for i in devices if i - distance in devices]
    return lax.ppermute(block, axis, route)


def angle_pair(index, points):
    angles = (index % points).astype(jnp.float32) * (2.0 * math.pi / points)
    return jnp.cos(angles), jnp.sin(angles)


def window_of(time_index, points):
    return 0.5 - 0.5 * jnp.cos(time_index.astype(jnp.float32) * (2.0 * math.pi / points))


def analysis_table(points):
    halfway = points // 2
    lanes = min(128, halfway)
    groups = halfway // lanes
    time_index = jnp.arange(points, dtype=jnp.int32)[None, :]
    fine = angle_pair(jnp.arange(lanes, dtype=jnp.int32)[:, None] * time_index, points)
    row = jnp.arange(2 * groups, dtype=jnp.int32)[:, None]
    is_sine = row >= groups
    coarse_cos, coarse_sin = angle_pair(((row % groups) * lanes) * time_index, points)
    first = jnp.where(is_sine, -coarse_sin, coarse_cos)
    second = jnp.where(is_sine, -coarse_cos, -coarse_sin)
    scale = window_of(time_index, points) * (1.0 / math.sqrt(points))
    fine_cos, fine_sin = (part * scale for part in fine)
    entry_value = first[:, None, :] * fine_cos[None, :, :] + second[:, None, :] * fine_sin[None, :, :]
    table = entry_value.astype(jnp.bfloat16)
    return lax.optimization_barrier(table.reshape(points, points))


def synthesis_rows(first_bin, band_count):
    sub = 16 if band_count % 16 == 0 else 1
    time_index = jnp.arange(NFFT, dtype=jnp.int32)[None, :]
    row = jnp.arange(2 * (band_count // sub), dtype=jnp.int32)[:, None]
    is_sine = row >= band_count // sub
    coarse_bins = first_bin + sub * (row % (band_count // sub))
    coarse_cos, coarse_sin = angle_pair(coarse_bins * time_index, NFFT)
    scale = window_of(time_index, NFFT) * (1.0 / math.sqrt(BINS))
    fine_cos, fine_sin = (
        part * scale
        for part in angle_pair(jnp.arange(sub, dtype=jnp.int32)[:, None] * time_index, NFFT)
    )
    first = jnp.where(is_sine, -coarse_sin, coarse_cos)
    second = jnp.where(is_sine, -coarse_cos, -coarse_sin)
    entry_value = first[:, None, :] * fine_cos[None, :, :] + second[:, None, :] * fine_sin[None, :, :]
    table = entry_value.astype(jnp.bfloat16)
    return lax.optimization_barrier(table.reshape(2, band_count, NFFT))


def gathered_sum(value, axis):
    size = lax.axis_size(axis)
    here = lax.axis_index(axis)
    devices = range(size)
    slots = jnp.zeros((size,) + value.shape, value.dtype)
    for distance in range(size):
        if distance == 0:
            arrived = value
        else:
            route = [(i, (i + distance) % size) for i in devices]
            arrived = lax.ppermute(value, axis, route)
        source = (here - distance) % size
        slots = slots + jnp.where(
            (jnp.arange(size, dtype=jnp.int32) == source).reshape((size,) + (1,) * value.ndim),
            arrived[None],
            0.0,
        )
    return jnp.sum(slots, axis=0)


def spread_parts(quarters):
    return sum(
        (
            jnp.pad(quarters[:, :, quarter], ((0, 0), (quarter, 3 - quarter), (0, 0)))
            for quarter in range(4)
        )
    )


def framed(signal, beyond, stride):
    frame_count = signal.shape[1] // stride
    padded = jnp.concatenate([signal, beyond], axis=1).reshape(
        signal.shape[0], frame_count + 3, stride
    )
    return jnp.concatenate(
        [padded[:, quarter : quarter + frame_count] for quarter in range(4)], axis=2
    )


def body(spectra, target, lengths):
    clip_count = spectra.shape[0]
    band_count = spectra.shape[2]
    frames_all = spectra.shape[3]
    samples = target.shape[1]
    rows_here = samples // HOP
    seg_index = lax.axis_index("seg")
    start_sample = seg_index * samples
    local_table = synthesis_rows(seg_index * band_count, band_count)
    sample_index = start_sample + jnp.arange(samples, dtype=jnp.int32)
    inside = sample_index[None, :] < (lengths * HOP)[:, None]
    clean = jnp.where(inside, target, jnp.zeros_like(target))
    clean, local_table = lax.optimization_barrier((clean, local_table))
    padded_spec = jnp.pad(spectra, ((0, 0), (0, 0), (0, 0), (3, 0)))
    framed_sig = jnp.einsum(
        "crbf,rbm->fcm", padded_spec, local_table, preferred_element_type=jnp.float32
    )
    hop_rows = lax.psum_scatter(
        sum(
            (
                framed_sig[
                    3 - quarter : 3 - quarter + rows_here * lax.axis_size("seg"),
                    :,
                    quarter * HOP : (quarter + 1) * HOP,
                ]
                for quarter in range(4)
            )
        ),
        "seg",
        scatter_dimension=0,
        tiled=True,
    )
    estimate = jnp.transpose(hop_rows, (1, 0, 2)).reshape(clip_count, samples)
    est_wave = jnp.where(inside, estimate, 0.0).astype(jnp.bfloat16)
    sizes_list = (NFFT // 4, NFFT // 2, NFFT)
    halo = 3 * NFFT // 4
    clean_beyond = shifted(clean[:, :halo], "seg", -1)
    est_beyond = shifted(est_wave[:, :halo], "seg", -1)
    saved = []
    spread_list = []
    energy_list = []
    logterm_list = []
    for points in sizes_list:
        stride = points // 4
        halfway = points // 2
        frame_count = samples // stride
        table = analysis_table(points)
        tgt_x = jnp.einsum(
            "cfm,jm->cfj",
            framed(clean, clean_beyond[:, : 3 * stride], stride),
            table,
            preferred_element_type=jnp.float32,
        )
        est_x = jnp.einsum(
            "cfm,jm->cfj",
            framed(est_wave, est_beyond[:, : 3 * stride], stride),
            table,
            preferred_element_type=jnp.float32,
        )
        est_real = est_x[:, :, :halfway]
        est_imag = est_x[:, :, halfway:]
        tgt_real = tgt_x[:, :, :halfway]
        tgt_imag = tgt_x[:, :, halfway:]
        est_mag = jnp.sqrt(est_real * est_real + est_imag * est_imag + EPS_MAG)
        tgt_mag = jnp.sqrt(tgt_real * tgt_real + tgt_imag * tgt_imag + EPS_MAG)
        usable_count = lengths * (HOP // stride)
        frame_index = start_sample // stride + jnp.arange(frame_count, dtype=jnp.int32)
        usable = frame_index[None, :, None] < usable_count[:, None, None]
        mag_gap = est_mag - tgt_mag
        log_gap = jnp.log(est_mag) - jnp.log(tgt_mag)
        entries = (usable_count * halfway).astype(jnp.float32)
        spread_list.append(jnp.sum(jnp.where(usable, mag_gap * mag_gap, 0.0), axis=(1, 2)))
        energy_list.append(jnp.sum(jnp.where(usable, tgt_mag * tgt_mag, 0.0), axis=(1, 2)))
        logterm_list.append(
            jnp.sum(jnp.where(usable, log_gap * log_gap, 0.0), axis=(1, 2)) / entries
        )
        saved.append((est_real, est_imag, est_mag, mag_gap, log_gap, usable, entries, table))
    spreads = jnp.stack(spread_list)
    energies = jnp.stack(energy_list)
    logterms = jnp.stack(logterm_list)
    parts = lax.all_gather(jnp.stack([spreads, energies, logterms]), "seg", axis=0, tiled=False)
    spreads, energies, logterms = jnp.sum(parts, axis=0)
    own_loss = jnp.sum(jnp.sqrt((spreads + EPS_RATIO) / energies) + logterms)
    clip_groups = lax.axis_size("clip")
    seg_count = lax.axis_size("seg")
    carried = 1 < clip_groups <= seg_count + 1
    if carried:
        lag = [1 + s % (clip_groups - 1) for s in range(seg_count)]
        route = [
            (c * seg_count + s, ((c + lag[s]) % clip_groups) * seg_count + s)
            for c in range(clip_groups)
            for s in range(seg_count)
        ]
        loss_received = lax.ppermute(own_loss, ("clip", "seg"), route)
    else:
        loss = gathered_sum(own_loss, "clip") / (3 * clip_count * clip_groups)
    ratio_weight = 1.0 / jnp.sqrt((spreads + EPS_RATIO) * energies)
    gradient = jnp.zeros((clip_count, samples), jnp.float32)
    extras = []
    for level, points in enumerate(sizes_list):
        stride = points // 4
        frame_count = samples // stride
        est_real, est_imag, est_mag, mag_gap, log_gap, usable, entries, table = saved[level]
        grad_mag = jnp.where(
            usable,
            mag_gap * ratio_weight[level][:, None, None]
            + 2.0 * log_gap / (est_mag * entries[:, None, None]),
            0.0,
        ) * (frames_all * BINS)
        grad_x = jnp.concatenate(
            [grad_mag * est_real / est_mag, grad_mag * est_imag / est_mag], axis=2
        ).astype(jnp.bfloat16)
        grad_frames = jnp.einsum(
            "cfj,jm->cfm", grad_x, table, preferred_element_type=jnp.float32
        )
        spread_back = spread_parts(grad_frames.reshape(clip_count, frame_count, 4, stride))
        gradient = gradient + spread_back[:, :frame_count].reshape(clip_count, samples)
        extras.append(spread_back[:, frame_count:].reshape(clip_count, 3 * stride))
    halo = 3 * NFFT // 4
    spill = sum(jnp.pad(extra, ((0, 0), (0, halo - extra.shape[1]))) for extra in extras)
    received = shifted(spill, "seg", 1)
    gradient = gradient + jnp.pad(received, ((0, 0), (0, samples - halo)))
    grad_wave = jnp.where(inside, gradient, 0.0).astype(jnp.bfloat16)
    grad_hops = grad_wave.reshape(clip_count, rows_here, HOP)
    if carried:
        high = loss_received.astype(jnp.bfloat16)
        low = (loss_received - high.astype(jnp.float32)).astype(jnp.bfloat16)
        lane = jnp.arange(HOP, dtype=jnp.int32)
        carrier = jnp.where(lane == 0, high, jnp.where(lane == 1, low, jnp.zeros((), jnp.bfloat16)))
        carrier = jnp.broadcast_to(carrier[None, None, :], (1, rows_here, HOP))
        gathered = lax.all_gather(
            jnp.concatenate([grad_hops, carrier], axis=0), "seg", axis=1, tiled=True
        )
        portion = gathered[:clip_count]
        peer_pairs = gathered[clip_count, ::rows_here, :2]
        own_high = own_loss.astype(jnp.bfloat16)
        own_low = (own_loss - own_high.astype(jnp.float32)).astype(jnp.bfloat16)
        own_value = own_high.astype(jnp.float32) + own_low.astype(jnp.float32)
        peer_values = peer_pairs[:, 0].astype(jnp.float32) + peer_pairs[:, 1].astype(jnp.float32)
        clip_index = lax.axis_index("clip")
        group_losses = []
        for group in range(clip_groups):
            behind = (clip_index - group) % clip_groups
            from_peer = jnp.sum(
                jnp.where(jnp.arange(seg_count) == jnp.maximum(behind - 1, 0), peer_values, 0.0)
            )
            group_losses.append(jnp.where(behind == 0, own_value, from_peer))
        loss = sum(group_losses) / (3 * clip_count * clip_groups)
    else:
        portion = lax.all_gather(grad_hops, "seg", axis=1, tiled=True)
    padded = jnp.concatenate([portion, jnp.zeros((clip_count, 3, HOP), portion.dtype)], axis=1)
    grad_signals = jnp.concatenate(
        [padded[:, quarter : quarter + frames_all] for quarter in range(4)], axis=2
    )
    spec_grad = jnp.einsum(
        "ctm,rbm->crbt", grad_signals, local_table, preferred_element_type=jnp.float32
    ).astype(jnp.bfloat16)
    return (loss, spec_grad)


def solution(mesh):
    return jax.shard_map(
        body,
        mesh=mesh,
        in_specs=(P("clip", None, "seg", None), P("clip", "seg"), P("clip")),
        out_specs=(P(), P("clip", None, "seg", None)),
        check_vma=False,
    )
```

```python
import math

import jax
import jax.numpy as jnp
from jax import lax
from jax.sharding import PartitionSpec as P

BINS = 1024
NFFT = 2048
HOP = 512


EPS_MAG = 0.1
EPS_RATIO = 1e-05


def shifted(block, axis, distance):
    devices = range(lax.axis_size(axis))
    route = [(i - distance, i) for i in devices if i - distance in devices]
    return lax.ppermute(block, axis, route)


def angle_pair(index, points):
    angles = (index % points).astype(jnp.float32) * (2.0 * math.pi / points)
    return jnp.cos(angles), jnp.sin(angles)


def window_of(time_index, points):
    return 0.5 - 0.5 * jnp.cos(time_index.astype(jnp.float32) * (2.0 * math.pi / points))


def analysis_table(points):
    halfway = points // 2
    lanes = min(128, halfway)
    groups = halfway // lanes
    time_index = jnp.arange(points, dtype=jnp.int32)[None, :]
    fine = angle_pair(jnp.arange(lanes, dtype=jnp.int32)[:, None] * time_index, points)
    row = jnp.arange(2 * groups, dtype=jnp.int32)[:, None]
    is_sine = row >= groups
    coarse_cos, coarse_sin = angle_pair(((row % groups) * lanes) * time_index, points)
    first = jnp.where(is_sine, -coarse_sin, coarse_cos)
    second = jnp.where(is_sine, -coarse_cos, -coarse_sin)
    scale = window_of(time_index, points) * (1.0 / math.sqrt(points))
    fine_cos, fine_sin = (part * scale for part in fine)
    entry_value = first[:, None, :] * fine_cos[None, :, :] + second[:, None, :] * fine_sin[None, :, :]
    table = entry_value.astype(jnp.bfloat16)
    return lax.optimization_barrier(table.reshape(points, points))


def synthesis_rows(first_bin, band_count):
    sub = 16 if band_count % 16 == 0 else 1
    time_index = jnp.arange(NFFT, dtype=jnp.int32)[None, :]
    row = jnp.arange(2 * (band_count // sub), dtype=jnp.int32)[:, None]
    is_sine = row >= band_count // sub
    coarse_bins = first_bin + sub * (row % (band_count // sub))
    coarse_cos, coarse_sin = angle_pair(coarse_bins * time_index, NFFT)
    scale = window_of(time_index, NFFT) * (1.0 / math.sqrt(BINS))
    fine_cos, fine_sin = (
        part * scale
        for part in angle_pair(jnp.arange(sub, dtype=jnp.int32)[:, None] * time_index, NFFT)
    )
    first = jnp.where(is_sine, -coarse_sin, coarse_cos)
    second = jnp.where(is_sine, -coarse_cos, -coarse_sin)
    entry_value = first[:, None, :] * fine_cos[None, :, :] + second[:, None, :] * fine_sin[None, :, :]
    table = entry_value.astype(jnp.bfloat16)
    return lax.optimization_barrier(table.reshape(2, band_count, NFFT))


def gathered_sum(value, axis):
    size = lax.axis_size(axis)
    here = lax.axis_index(axis)
    held = [value]
    for distance in range(1, size):
        route = [(i, (i + distance) % size) for i in range(size)]
        held.append(lax.ppermute(value, axis, route))
    in_order = jnp.take(jnp.stack(held), (here - jnp.arange(size, dtype=jnp.int32)) % size, axis=0)
    return jnp.sum(in_order, axis=0)


def spread_parts(quarters):
    return sum(
        (
            jnp.pad(quarters[:, :, quarter], ((0, 0), (quarter, 3 - quarter), (0, 0)))
            for quarter in range(4)
        )
    )


def framed(signal, beyond, stride):
    frame_count = signal.shape[1] // stride
    padded = jnp.concatenate([signal, beyond], axis=1).reshape(
        signal.shape[0], frame_count + 3, stride
    )
    return jnp.concatenate(
        [padded[:, quarter : quarter + frame_count] for quarter in range(4)], axis=2
    )


def body(spectra, target, lengths):
    clip_count = spectra.shape[0]
    band_count = spectra.shape[2]
    frames_all = spectra.shape[3]
    samples = target.shape[1]
    rows_here = samples // HOP
    seg_index = lax.axis_index("seg")
    start_sample = seg_index * samples
    local_table = synthesis_rows(seg_index * band_count, band_count)
    sample_index = start_sample + jnp.arange(samples, dtype=jnp.int32)
    inside = sample_index[None, :] < (lengths * HOP)[:, None]
    clean = jnp.where(inside, target, jnp.zeros_like(target))
    clean, local_table = lax.optimization_barrier((clean, local_table))
    padded_spec = jnp.pad(spectra, ((0, 0), (0, 0), (0, 0), (3, 0)))
    framed_sig = jnp.einsum(
        "crbf,rbm->fcm", padded_spec, local_table, preferred_element_type=jnp.float32
    )
    hop_rows = lax.psum_scatter(
        sum(
            (
                framed_sig[
                    3 - quarter : 3 - quarter + rows_here * lax.axis_size("seg"),
                    :,
                    quarter * HOP : (quarter + 1) * HOP,
                ]
                for quarter in range(4)
            )
        ),
        "seg",
        scatter_dimension=0,
        tiled=True,
    )
    estimate = jnp.transpose(hop_rows, (1, 0, 2)).reshape(clip_count, samples)
    est_wave = jnp.where(inside, estimate, 0.0).astype(jnp.bfloat16)
    sizes_list = (NFFT // 4, NFFT // 2, NFFT)
    halo = 3 * NFFT // 4
    clean_beyond = shifted(clean[:, :halo], "seg", -1)
    est_beyond = shifted(est_wave[:, :halo], "seg", -1)
    saved = []
    spread_list = []
    energy_list = []
    logterm_list = []
    for points in sizes_list:
        stride = points // 4
        halfway = points // 2
        frame_count = samples // stride
        table = analysis_table(points)
        tgt_x = jnp.einsum(
            "cfm,jm->cfj",
            framed(clean, clean_beyond[:, : 3 * stride], stride),
            table,
            preferred_element_type=jnp.float32,
        )
        est_x = jnp.einsum(
            "cfm,jm->cfj",
            framed(est_wave, est_beyond[:, : 3 * stride], stride),
            table,
            preferred_element_type=jnp.float32,
        )
        est_real = est_x[:, :, :halfway]
        est_imag = est_x[:, :, halfway:]
        tgt_real = tgt_x[:, :, :halfway]
        tgt_imag = tgt_x[:, :, halfway:]
        est_mag = jnp.sqrt(est_real * est_real + est_imag * est_imag + EPS_MAG)
        tgt_mag = jnp.sqrt(tgt_real * tgt_real + tgt_imag * tgt_imag + EPS_MAG)
        usable_count = lengths * (HOP // stride)
        frame_index = start_sample // stride + jnp.arange(frame_count, dtype=jnp.int32)
        usable = frame_index[None, :, None] < usable_count[:, None, None]
        mag_gap = est_mag - tgt_mag
        log_gap = jnp.log(est_mag) - jnp.log(tgt_mag)
        entries = (usable_count * halfway).astype(jnp.float32)
        spread_list.append(jnp.sum(jnp.where(usable, mag_gap * mag_gap, 0.0), axis=(1, 2)))
        energy_list.append(jnp.sum(jnp.where(usable, tgt_mag * tgt_mag, 0.0), axis=(1, 2)))
        logterm_list.append(
            jnp.sum(jnp.where(usable, log_gap * log_gap, 0.0), axis=(1, 2)) / entries
        )
        saved.append((est_real, est_imag, est_mag, mag_gap, log_gap, usable, entries, table))
    spreads = jnp.stack(spread_list)
    energies = jnp.stack(energy_list)
    logterms = jnp.stack(logterm_list)
    parts = lax.all_gather(jnp.stack([spreads, energies, logterms]), "seg", axis=0, tiled=False)
    spreads, energies, logterms = jnp.sum(parts, axis=0)
    own_loss = jnp.sum(jnp.sqrt((spreads + EPS_RATIO) / energies) + logterms)
    loss = gathered_sum(own_loss, "clip") / (3 * clip_count * lax.axis_size("clip"))
    ratio_weight = 1.0 / jnp.sqrt((spreads + EPS_RATIO) * energies)
    gradient = jnp.zeros((clip_count, samples), jnp.float32)
    extras = []
    for level, points in enumerate(sizes_list):
        stride = points // 4
        frame_count = samples // stride
        est_real, est_imag, est_mag, mag_gap, log_gap, usable, entries, table = saved[level]
        grad_mag = jnp.where(
            usable,
            mag_gap * ratio_weight[level][:, None, None]
            + 2.0 * log_gap / (est_mag * entries[:, None, None]),
            0.0,
        ) * (frames_all * BINS)
        grad_x = jnp.concatenate(
            [grad_mag * est_real / est_mag, grad_mag * est_imag / est_mag], axis=2
        ).astype(jnp.bfloat16)
        grad_frames = jnp.einsum(
            "cfj,jm->cfm", grad_x, table, preferred_element_type=jnp.float32
        )
        spread_back = spread_parts(grad_frames.reshape(clip_count, frame_count, 4, stride))
        gradient = gradient + spread_back[:, :frame_count].reshape(clip_count, samples)
        extras.append(spread_back[:, frame_count:].reshape(clip_count, 3 * stride))
    halo = 3 * NFFT // 4
    spill = sum(jnp.pad(extra, ((0, 0), (0, halo - extra.shape[1]))) for extra in extras)
    received = shifted(spill, "seg", 1)
    gradient = gradient + jnp.pad(received, ((0, 0), (0, samples - halo)))
    grad_wave = jnp.where(inside, gradient, 0.0).astype(jnp.bfloat16)
    grad_hops = grad_wave.reshape(clip_count, rows_here, HOP)
    portion = lax.all_gather(grad_hops, "seg", axis=1, tiled=True)
    padded = jnp.concatenate([portion, jnp.zeros((clip_count, 3, HOP), portion.dtype)], axis=1)
    grad_signals = jnp.concatenate(
        [padded[:, quarter : quarter + frames_all] for quarter in range(4)], axis=2
    )
    spec_grad = jnp.einsum(
        "ctm,rbm->crbt", grad_signals, local_table, preferred_element_type=jnp.float32
    ).astype(jnp.bfloat16)
    return (loss, spec_grad)


def solution(mesh):
    return jax.shard_map(
        body,
        mesh=mesh,
        in_specs=(P("clip", None, "seg", None), P("clip", "seg"), P("clip")),
        out_specs=(P(), P("clip", None, "seg", None)),
        check_vma=False,
    )
```

```python
import math

import jax
import jax.numpy as jnp
from jax import lax
from jax.sharding import PartitionSpec as P

BINS = 1024
NFFT = 2048
HOP = 512


EPS_MAG = 0.1
EPS_RATIO = 1e-05


def shifted(block, axis, distance):
    devices = range(lax.axis_size(axis))
    route = [(i - distance, i) for i in devices if i - distance in devices]
    return lax.ppermute(block, axis, route)


def angle_pair(index, points):
    angles = (index % points).astype(jnp.float32) * (2.0 * math.pi / points)
    return jnp.cos(angles), jnp.sin(angles)


def window_of(time_index, points):
    return 0.5 - 0.5 * jnp.cos(time_index.astype(jnp.float32) * (2.0 * math.pi / points))


def analysis_table(points):
    halfway = points // 2
    lanes = min(128, halfway)
    groups = halfway // lanes
    time_index = jnp.arange(points, dtype=jnp.int32)[None, :]
    fine = angle_pair(jnp.arange(lanes, dtype=jnp.int32)[:, None] * time_index, points)
    row = jnp.arange(2 * groups, dtype=jnp.int32)[:, None]
    is_sine = row >= groups
    coarse_cos, coarse_sin = angle_pair(((row % groups) * lanes) * time_index, points)
    first = jnp.where(is_sine, -coarse_sin, coarse_cos)
    second = jnp.where(is_sine, -coarse_cos, -coarse_sin)
    scale = window_of(time_index, points) * (1.0 / math.sqrt(points))
    fine_cos, fine_sin = (part * scale for part in fine)
    entry_value = first[:, None, :] * fine_cos[None, :, :] + second[:, None, :] * fine_sin[None, :, :]
    table = entry_value.astype(jnp.bfloat16)
    return lax.optimization_barrier(table.reshape(points, points))


def synthesis_rows(first_bin, band_count):
    sub = 16 if band_count % 16 == 0 else 1
    time_index = jnp.arange(NFFT, dtype=jnp.int32)[None, :]
    row = jnp.arange(2 * (band_count // sub), dtype=jnp.int32)[:, None]
    is_sine = row >= band_count // sub
    coarse_bins = first_bin + sub * (row % (band_count // sub))
    coarse_cos, coarse_sin = angle_pair(coarse_bins * time_index, NFFT)
    scale = window_of(time_index, NFFT) * (1.0 / math.sqrt(BINS))
    fine_cos, fine_sin = (
        part * scale
        for part in angle_pair(jnp.arange(sub, dtype=jnp.int32)[:, None] * time_index, NFFT)
    )
    first = jnp.where(is_sine, -coarse_sin, coarse_cos)
    second = jnp.where(is_sine, -coarse_cos, -coarse_sin)
    entry_value = first[:, None, :] * fine_cos[None, :, :] + second[:, None, :] * fine_sin[None, :, :]
    table = entry_value.astype(jnp.bfloat16)
    return lax.optimization_barrier(table.reshape(2, band_count, NFFT))


def gathered_sum(value, axis):
    size = lax.axis_size(axis)
    here = lax.axis_index(axis)
    devices = range(size)
    slots = jnp.zeros((size,) + value.shape, value.dtype)
    for distance in range(size):
        if distance == 0:
            arrived = value
        else:
            route = [(i, (i + distance) % size) for i in devices]
            arrived = lax.ppermute(value, axis, route)
        source = (here - distance) % size
        slots = slots + jnp.where(
            (jnp.arange(size, dtype=jnp.int32) == source).reshape((size,) + (1,) * value.ndim),
            arrived[None],
            0.0,
        )
    return jnp.sum(slots, axis=0)


def spread_parts(frames, stride):
    return sum(
        (
            jnp.pad(
                frames[:, :, quarter * stride : (quarter + 1) * stride],
                ((0, 0), (quarter, 3 - quarter), (0, 0)),
            )
            for quarter in range(4)
        )
    )


def framed(signal, beyond, stride):
    frame_count = signal.shape[1] // stride
    padded = jnp.concatenate([signal, beyond], axis=1).reshape(
        signal.shape[0], frame_count + 3, stride
    )
    return jnp.concatenate(
        [padded[:, quarter : quarter + frame_count] for quarter in range(4)], axis=2
    )


def body(spectra, target, lengths):
    clip_count = spectra.shape[0]
    band_count = spectra.shape[2]
    frames_all = spectra.shape[3]
    samples = target.shape[1]
    rows_here = samples // HOP
    seg_index = lax.axis_index("seg")
    start_sample = seg_index * samples
    local_table = synthesis_rows(seg_index * band_count, band_count)
    sample_index = start_sample + jnp.arange(samples, dtype=jnp.int32)
    inside = sample_index[None, :] < (lengths * HOP)[:, None]
    clean = jnp.where(inside, target, jnp.zeros_like(target))
    clean, local_table = lax.optimization_barrier((clean, local_table))
    padded_spec = jnp.pad(spectra, ((0, 0), (0, 0), (0, 0), (3, 0)))
    framed_sig = jnp.einsum(
        "crbf,rbm->fcm", padded_spec, local_table, preferred_element_type=jnp.float32
    )
    hop_rows = lax.psum_scatter(
        sum(
            (
                framed_sig[
                    3 - quarter : 3 - quarter + rows_here * lax.axis_size("seg"),
                    :,
                    quarter * HOP : (quarter + 1) * HOP,
                ]
                for quarter in range(4)
            )
        ),
        "seg",
        scatter_dimension=0,
        tiled=True,
    )
    estimate = jnp.transpose(hop_rows, (1, 0, 2)).reshape(clip_count, samples)
    est_wave = jnp.where(inside, estimate, 0.0).astype(jnp.bfloat16)
    sizes_list = (NFFT // 4, NFFT // 2, NFFT)
    halo = 3 * NFFT // 4
    clean_beyond = shifted(clean[:, :halo], "seg", -1)
    est_beyond = shifted(est_wave[:, :halo], "seg", -1)
    saved = []
    spread_list = []
    energy_list = []
    logterm_list = []
    for points in sizes_list:
        stride = points // 4
        halfway = points // 2
        frame_count = samples // stride
        table = analysis_table(points)
        tgt_x = jnp.einsum(
            "cfm,jm->cfj",
            framed(clean, clean_beyond[:, : 3 * stride], stride),
            table,
            preferred_element_type=jnp.float32,
        )
        est_x = jnp.einsum(
            "cfm,jm->cfj",
            framed(est_wave, est_beyond[:, : 3 * stride], stride),
            table,
            preferred_element_type=jnp.float32,
        )
        est_real = est_x[:, :, :halfway]
        est_imag = est_x[:, :, halfway:]
        tgt_real = tgt_x[:, :, :halfway]
        tgt_imag = tgt_x[:, :, halfway:]
        est_mag = jnp.sqrt(est_real * est_real + est_imag * est_imag + EPS_MAG)
        tgt_mag = jnp.sqrt(tgt_real * tgt_real + tgt_imag * tgt_imag + EPS_MAG)
        usable_count = lengths * (HOP // stride)
        frame_index = start_sample // stride + jnp.arange(frame_count, dtype=jnp.int32)
        usable = frame_index[None, :, None] < usable_count[:, None, None]
        mag_gap = est_mag - tgt_mag
        log_gap = jnp.log(est_mag) - jnp.log(tgt_mag)
        entries = (usable_count * halfway).astype(jnp.float32)
        spread_list.append(jnp.sum(jnp.where(usable, mag_gap * mag_gap, 0.0), axis=(1, 2)))
        energy_list.append(jnp.sum(jnp.where(usable, tgt_mag * tgt_mag, 0.0), axis=(1, 2)))
        logterm_list.append(
            jnp.sum(jnp.where(usable, log_gap * log_gap, 0.0), axis=(1, 2)) / entries
        )
        saved.append((est_real, est_imag, est_mag, mag_gap, log_gap, usable, entries, table))
    spreads = jnp.stack(spread_list)
    energies = jnp.stack(energy_list)
    logterms = jnp.stack(logterm_list)
    parts = lax.all_gather(jnp.stack([spreads, energies, logterms]), "seg", axis=0, tiled=False)
    spreads, energies, logterms = jnp.sum(parts, axis=0)
    own_loss = jnp.sum(jnp.sqrt((spreads + EPS_RATIO) / energies) + logterms)
    loss = gathered_sum(own_loss, "clip") / (3 * clip_count * lax.axis_size("clip"))
    ratio_weight = 1.0 / jnp.sqrt((spreads + EPS_RATIO) * energies)
    gradient = jnp.zeros((clip_count, samples), jnp.float32)
    extras = []
    for level, points in enumerate(sizes_list):
        stride = points // 4
        frame_count = samples // stride
        est_real, est_imag, est_mag, mag_gap, log_gap, usable, entries, table = saved[level]
        grad_mag = jnp.where(
            usable,
            mag_gap * ratio_weight[level][:, None, None]
            + 2.0 * log_gap / (est_mag * entries[:, None, None]),
            0.0,
        ) * (frames_all * BINS)
        grad_x = jnp.concatenate(
            [grad_mag * est_real / est_mag, grad_mag * est_imag / est_mag], axis=2
        ).astype(jnp.bfloat16)
        grad_frames = jnp.einsum(
            "cfj,jm->cfm", grad_x, table, preferred_element_type=jnp.float32
        )
        spread_back = spread_parts(grad_frames, stride)
        gradient = gradient + spread_back[:, :frame_count].reshape(clip_count, samples)
        extras.append(spread_back[:, frame_count:].reshape(clip_count, 3 * stride))
    halo = 3 * NFFT // 4
    spill = sum(jnp.pad(extra, ((0, 0), (0, halo - extra.shape[1]))) for extra in extras)
    received = shifted(spill, "seg", 1)
    gradient = gradient + jnp.pad(received, ((0, 0), (0, samples - halo)))
    grad_wave = jnp.where(inside, gradient, 0.0).astype(jnp.bfloat16)
    grad_hops = grad_wave.reshape(clip_count, rows_here, HOP)
    portion = lax.all_gather(grad_hops, "seg", axis=1, tiled=True)
    padded = jnp.concatenate([portion, jnp.zeros((clip_count, 3, HOP), portion.dtype)], axis=1)
    grad_signals = jnp.concatenate(
        [padded[:, quarter : quarter + frames_all] for quarter in range(4)], axis=2
    )
    spec_grad = jnp.einsum(
        "ctm,rbm->crbt", grad_signals, local_table, preferred_element_type=jnp.float32
    ).astype(jnp.bfloat16)
    return (loss, spec_grad)


def solution(mesh):
    return jax.shard_map(
        body,
        mesh=mesh,
        in_specs=(P("clip", None, "seg", None), P("clip", "seg"), P("clip")),
        out_specs=(P(), P("clip", None, "seg", None)),
        check_vma=False,
    )
```

```python
import math

import jax
import jax.numpy as jnp
from jax import lax
from jax.sharding import PartitionSpec as P

BINS = 1024
NFFT = 2048
HOP = 512


EPS_MAG = 0.1
EPS_RATIO = 1e-05


def shifted(block, axis, distance):
    devices = range(lax.axis_size(axis))
    route = [(i - distance, i) for i in devices if i - distance in devices]
    return lax.ppermute(block, axis, route)


def angle_pair(index, points):
    angles = (index % points).astype(jnp.float32) * (2.0 * math.pi / points)
    return jnp.cos(angles), jnp.sin(angles)


def window_of(time_index, points):
    return 0.5 - 0.5 * jnp.cos(time_index.astype(jnp.float32) * (2.0 * math.pi / points))


def analysis_table(points):
    halfway = points // 2
    lanes = min(128, halfway)
    groups = halfway // lanes
    time_index = jnp.arange(points, dtype=jnp.int32)[None, :]
    fine = angle_pair(jnp.arange(lanes, dtype=jnp.int32)[:, None] * time_index, points)
    row = jnp.arange(2 * groups, dtype=jnp.int32)[:, None]
    is_sine = row >= groups
    coarse_cos, coarse_sin = angle_pair(((row % groups) * lanes) * time_index, points)
    first = jnp.where(is_sine, -coarse_sin, coarse_cos)
    second = jnp.where(is_sine, -coarse_cos, -coarse_sin)
    scale = window_of(time_index, points) * (1.0 / math.sqrt(points))
    fine_cos, fine_sin = (part * scale for part in fine)
    entry_value = first[:, None, :] * fine_cos[None, :, :] + second[:, None, :] * fine_sin[None, :, :]
    table = entry_value.astype(jnp.bfloat16)
    return lax.optimization_barrier(table.reshape(points, points))


def synthesis_rows(first_bin, band_count):
    sub = 16 if band_count % 16 == 0 else 1
    time_index = jnp.arange(NFFT, dtype=jnp.int32)[None, :]
    row = jnp.arange(2 * (band_count // sub), dtype=jnp.int32)[:, None]
    is_sine = row >= band_count // sub
    coarse_bins = first_bin + sub * (row % (band_count // sub))
    coarse_cos, coarse_sin = angle_pair(coarse_bins * time_index, NFFT)
    scale = window_of(time_index, NFFT) * (1.0 / math.sqrt(BINS))
    fine_cos, fine_sin = (
        part * scale
        for part in angle_pair(jnp.arange(sub, dtype=jnp.int32)[:, None] * time_index, NFFT)
    )
    first = jnp.where(is_sine, -coarse_sin, coarse_cos)
    second = jnp.where(is_sine, -coarse_cos, -coarse_sin)
    entry_value = first[:, None, :] * fine_cos[None, :, :] + second[:, None, :] * fine_sin[None, :, :]
    table = entry_value.astype(jnp.bfloat16)
    return lax.optimization_barrier(table.reshape(2, band_count, NFFT))


def gathered_sum(value, axis):
    size = lax.axis_size(axis)
    here = lax.axis_index(axis)
    devices = range(size)
    slots = jnp.zeros((size,) + value.shape, value.dtype)
    for distance in range(size):
        if distance == 0:
            arrived = value
        else:
            route = [(i, (i + distance) % size) for i in devices]
            arrived = lax.ppermute(value, axis, route)
        source = (here - distance) % size
        slots = slots + jnp.where(
            (jnp.arange(size, dtype=jnp.int32) == source).reshape((size,) + (1,) * value.ndim),
            arrived[None],
            0.0,
        )
    return jnp.sum(slots, axis=0)


def spread_parts(frames, stride):
    return sum(
        (
            jnp.pad(
                frames[:, :, quarter * stride : (quarter + 1) * stride],
                ((0, 0), (quarter, 3 - quarter), (0, 0)),
            )
            for quarter in range(4)
        )
    )


def framed(signal, beyond, stride):
    frame_count = signal.shape[1] // stride
    padded = jnp.concatenate([signal, beyond], axis=1).reshape(
        signal.shape[0], frame_count + 3, stride
    )
    return jnp.concatenate(
        [padded[:, quarter : quarter + frame_count] for quarter in range(4)], axis=2
    )


def body(spectra, target, lengths):
    clip_count = spectra.shape[0]
    band_count = spectra.shape[2]
    frames_all = spectra.shape[3]
    samples = target.shape[1]
    rows_here = samples // HOP
    seg_index = lax.axis_index("seg")
    start_sample = seg_index * samples
    local_table = synthesis_rows(seg_index * band_count, band_count)
    sample_index = start_sample + jnp.arange(samples, dtype=jnp.int32)
    inside = sample_index[None, :] < (lengths * HOP)[:, None]
    clean = jnp.where(inside, target, jnp.zeros_like(target))
    clean, local_table = lax.optimization_barrier((clean, local_table))
    padded_spec = jnp.pad(spectra, ((0, 0), (0, 0), (0, 0), (3, 0)))
    framed_sig = jnp.einsum(
        "crbf,rbm->fcm", padded_spec, local_table, preferred_element_type=jnp.float32
    )
    hop_rows = lax.psum_scatter(
        sum(
            (
                framed_sig[
                    3 - quarter : 3 - quarter + rows_here * lax.axis_size("seg"),
                    :,
                    quarter * HOP : (quarter + 1) * HOP,
                ]
                for quarter in range(4)
            )
        ),
        "seg",
        scatter_dimension=0,
        tiled=True,
    )
    estimate = jnp.transpose(hop_rows, (1, 0, 2)).reshape(clip_count, samples)
    est_wave = jnp.where(inside, estimate, 0.0).astype(jnp.bfloat16)
    sizes_list = (NFFT // 4, NFFT // 2, NFFT)
    halo = 3 * NFFT // 4
    clean_beyond = shifted(clean[:, :halo], "seg", -1)
    est_beyond = shifted(est_wave[:, :halo], "seg", -1)
    saved = []
    spread_list = []
    energy_list = []
    logterm_list = []
    for points in sizes_list:
        stride = points // 4
        halfway = points // 2
        frame_count = samples // stride
        table = analysis_table(points)
        tgt_x = jnp.einsum(
            "cfm,jm->cfj",
            framed(clean, clean_beyond[:, : 3 * stride], stride),
            table,
            preferred_element_type=jnp.float32,
        )
        est_x = jnp.einsum(
            "cfm,jm->cfj",
            framed(est_wave, est_beyond[:, : 3 * stride], stride),
            table,
            preferred_element_type=jnp.float32,
        )
        est_real = est_x[:, :, :halfway]
        est_imag = est_x[:, :, halfway:]
        tgt_real = tgt_x[:, :, :halfway]
        tgt_imag = tgt_x[:, :, halfway:]
        est_mag = jnp.sqrt(est_real * est_real + est_imag * est_imag + EPS_MAG)
        tgt_mag = jnp.sqrt(tgt_real * tgt_real + tgt_imag * tgt_imag + EPS_MAG)
        usable_count = lengths * (HOP // stride)
        frame_index = start_sample // stride + jnp.arange(frame_count, dtype=jnp.int32)
        usable = frame_index[None, :, None] < usable_count[:, None, None]
        mag_gap = est_mag - tgt_mag
        log_gap = jnp.log(est_mag) - jnp.log(tgt_mag)
        entries = (usable_count * halfway).astype(jnp.float32)
        spread_list.append(jnp.sum(jnp.where(usable, mag_gap * mag_gap, 0.0), axis=(1, 2)))
        energy_list.append(jnp.sum(jnp.where(usable, tgt_mag * tgt_mag, 0.0), axis=(1, 2)))
        logterm_list.append(
            jnp.sum(jnp.where(usable, log_gap * log_gap, 0.0), axis=(1, 2)) / entries
        )
        saved.append((est_real, est_imag, est_mag, mag_gap, log_gap, usable, entries, table))
    spreads = jnp.stack(spread_list)
    energies = jnp.stack(energy_list)
    logterms = jnp.stack(logterm_list)
    parts = lax.all_gather(jnp.stack([spreads, energies, logterms]), "seg", axis=0, tiled=False)
    spreads, energies, logterms = jnp.sum(parts, axis=0)
    own_loss = jnp.sum(jnp.sqrt((spreads + EPS_RATIO) / energies) + logterms)
    loss = lax.psum(own_loss, "clip") / (3 * clip_count * lax.axis_size("clip"))
    ratio_weight = 1.0 / jnp.sqrt((spreads + EPS_RATIO) * energies)
    gradient = jnp.zeros((clip_count, samples), jnp.float32)
    extras = []
    for level, points in enumerate(sizes_list):
        stride = points // 4
        frame_count = samples // stride
        est_real, est_imag, est_mag, mag_gap, log_gap, usable, entries, table = saved[level]
        grad_mag = jnp.where(
            usable,
            mag_gap * ratio_weight[level][:, None, None]
            + 2.0 * log_gap / (est_mag * entries[:, None, None]),
            0.0,
        ) * (frames_all * BINS)
        grad_x = jnp.concatenate(
            [grad_mag * est_real / est_mag, grad_mag * est_imag / est_mag], axis=2
        ).astype(jnp.bfloat16)
        grad_frames = jnp.einsum(
            "cfj,jm->cfm", grad_x, table, preferred_element_type=jnp.float32
        )
        spread_back = spread_parts(grad_frames, stride)
        gradient = gradient + spread_back[:, :frame_count].reshape(clip_count, samples)
        extras.append(spread_back[:, frame_count:].reshape(clip_count, 3 * stride))
    halo = 3 * NFFT // 4
    spill = sum(jnp.pad(extra, ((0, 0), (0, halo - extra.shape[1]))) for extra in extras)
    received = shifted(spill, "seg", 1)
    gradient = gradient + jnp.pad(received, ((0, 0), (0, samples - halo)))
    grad_wave = jnp.where(inside, gradient, 0.0).astype(jnp.bfloat16)
    grad_hops = grad_wave.reshape(clip_count, rows_here, HOP)
    portion = lax.all_gather(grad_hops, "seg", axis=1, tiled=True)
    padded = jnp.concatenate([portion, jnp.zeros((clip_count, 3, HOP), portion.dtype)], axis=1)
    grad_signals = jnp.concatenate(
        [padded[:, quarter : quarter + frames_all] for quarter in range(4)], axis=2
    )
    spec_grad = jnp.einsum(
        "ctm,rbm->crbt", grad_signals, local_table, preferred_element_type=jnp.float32
    ).astype(jnp.bfloat16)
    return (loss, spec_grad)


def solution(mesh):
    return jax.shard_map(
        body,
        mesh=mesh,
        in_specs=(P("clip", None, "seg", None), P("clip", "seg"), P("clip")),
        out_specs=(P(), P("clip", None, "seg", None)),
        check_vma=False,
    )
```

```python
import math

import jax
import jax.numpy as jnp
from jax import lax
from jax.sharding import PartitionSpec as P

BINS = 1024
NFFT = 2048
HOP = 512


EPS_MAG = 0.1
EPS_RATIO = 1e-05


def shifted(block, axis, distance):
    devices = range(lax.axis_size(axis))
    route = [(i - distance, i) for i in devices if i - distance in devices]
    return lax.ppermute(block, axis, route)


def angle_pair(index, points):
    angles = (index % points).astype(jnp.float32) * (2.0 * math.pi / points)
    return jnp.cos(angles), jnp.sin(angles)


def window_of(time_index, points):
    return 0.5 - 0.5 * jnp.cos(time_index.astype(jnp.float32) * (2.0 * math.pi / points))


def analysis_table(points):
    halfway = points // 2
    lanes = min(128, halfway)
    groups = halfway // lanes
    time_index = jnp.arange(points, dtype=jnp.int32)[None, :]
    fine = angle_pair(jnp.arange(lanes, dtype=jnp.int32)[:, None] * time_index, points)
    row = jnp.arange(2 * groups, dtype=jnp.int32)[:, None]
    is_sine = row >= groups
    coarse_cos, coarse_sin = angle_pair(((row % groups) * lanes) * time_index, points)
    first = jnp.where(is_sine, -coarse_sin, coarse_cos)
    second = jnp.where(is_sine, -coarse_cos, -coarse_sin)
    scale = window_of(time_index, points) * (1.0 / math.sqrt(points))
    fine_cos, fine_sin = (part * scale for part in fine)
    entry_value = first[:, None, :] * fine_cos[None, :, :] + second[:, None, :] * fine_sin[None, :, :]
    table = entry_value.astype(jnp.bfloat16)
    return lax.optimization_barrier(table.reshape(points, points))


def synthesis_rows(first_bin, band_count):
    sub = 16 if band_count % 16 == 0 else 1
    time_index = jnp.arange(NFFT, dtype=jnp.int32)[None, :]
    row = jnp.arange(2 * (band_count // sub), dtype=jnp.int32)[:, None]
    is_sine = row >= band_count // sub
    coarse_bins = first_bin + sub * (row % (band_count // sub))
    coarse_cos, coarse_sin = angle_pair(coarse_bins * time_index, NFFT)
    scale = window_of(time_index, NFFT) * (1.0 / math.sqrt(BINS))
    fine_cos, fine_sin = (
        part * scale
        for part in angle_pair(jnp.arange(sub, dtype=jnp.int32)[:, None] * time_index, NFFT)
    )
    first = jnp.where(is_sine, -coarse_sin, coarse_cos)
    second = jnp.where(is_sine, -coarse_cos, -coarse_sin)
    entry_value = first[:, None, :] * fine_cos[None, :, :] + second[:, None, :] * fine_sin[None, :, :]
    table = entry_value.astype(jnp.bfloat16)
    return lax.optimization_barrier(table.reshape(2, band_count, NFFT))


def gathered_sum(value, axis):
    size = lax.axis_size(axis)
    here = lax.axis_index(axis)
    devices = range(size)
    slots = jnp.zeros((size,) + value.shape, value.dtype)
    for distance in range(size):
        if distance == 0:
            arrived = value
        else:
            route = [(i, (i + distance) % size) for i in devices]
            arrived = lax.ppermute(value, axis, route)
        source = (here - distance) % size
        slots = slots + jnp.where(
            (jnp.arange(size, dtype=jnp.int32) == source).reshape((size,) + (1,) * value.ndim),
            arrived[None],
            0.0,
        )
    return jnp.sum(slots, axis=0)


def spread_parts(frames, stride):
    return sum(
        (
            jnp.pad(
                frames[:, :, quarter * stride : (quarter + 1) * stride],
                ((0, 0), (quarter, 3 - quarter), (0, 0)),
            )
            for quarter in range(4)
        )
    )


def framed(signal, beyond, stride):
    frame_count = signal.shape[1] // stride
    padded = jnp.concatenate(
        [
            signal.reshape(signal.shape[0], frame_count, stride),
            beyond.reshape(signal.shape[0], 3, stride),
        ],
        axis=1,
    )
    return jnp.concatenate(
        [padded[:, quarter : quarter + frame_count] for quarter in range(4)], axis=2
    )


def body(spectra, target, lengths):
    clip_count = spectra.shape[0]
    band_count = spectra.shape[2]
    frames_all = spectra.shape[3]
    samples = target.shape[1]
    rows_here = samples // HOP
    seg_index = lax.axis_index("seg")
    start_sample = seg_index * samples
    local_table = synthesis_rows(seg_index * band_count, band_count)
    sample_index = start_sample + jnp.arange(samples, dtype=jnp.int32)
    inside = sample_index[None, :] < (lengths * HOP)[:, None]
    clean = jnp.where(inside, target, jnp.zeros_like(target))
    clean, local_table = lax.optimization_barrier((clean, local_table))
    padded_spec = jnp.pad(spectra, ((0, 0), (0, 0), (0, 0), (3, 0)))
    framed_sig = jnp.einsum(
        "crbf,rbm->fcm", padded_spec, local_table, preferred_element_type=jnp.float32
    )
    hop_rows = lax.psum_scatter(
        sum(
            (
                framed_sig[
                    3 - quarter : 3 - quarter + rows_here * lax.axis_size("seg"),
                    :,
                    quarter * HOP : (quarter + 1) * HOP,
                ]
                for quarter in range(4)
            )
        ),
        "seg",
        scatter_dimension=0,
        tiled=True,
    )
    estimate = jnp.transpose(hop_rows, (1, 0, 2)).reshape(clip_count, samples)
    est_wave = jnp.where(inside, estimate, 0.0).astype(jnp.bfloat16)
    sizes_list = (NFFT // 4, NFFT // 2, NFFT)
    halo = 3 * NFFT // 4
    clean_beyond = shifted(clean[:, :halo], "seg", -1)
    est_beyond = shifted(est_wave[:, :halo], "seg", -1)
    saved = []
    spread_list = []
    energy_list = []
    logterm_list = []
    for points in sizes_list:
        stride = points // 4
        halfway = points // 2
        frame_count = samples // stride
        table = analysis_table(points)
        tgt_x = jnp.einsum(
            "cfm,jm->cfj",
            framed(clean, clean_beyond[:, : 3 * stride], stride),
            table,
            preferred_element_type=jnp.float32,
        )
        est_x = jnp.einsum(
            "cfm,jm->cfj",
            framed(est_wave, est_beyond[:, : 3 * stride], stride),
            table,
            preferred_element_type=jnp.float32,
        )
        est_real = est_x[:, :, :halfway]
        est_imag = est_x[:, :, halfway:]
        tgt_real = tgt_x[:, :, :halfway]
        tgt_imag = tgt_x[:, :, halfway:]
        est_mag = jnp.sqrt(est_real * est_real + est_imag * est_imag + EPS_MAG)
        tgt_mag = jnp.sqrt(tgt_real * tgt_real + tgt_imag * tgt_imag + EPS_MAG)
        usable_count = lengths * (HOP // stride)
        frame_index = start_sample // stride + jnp.arange(frame_count, dtype=jnp.int32)
        usable = frame_index[None, :, None] < usable_count[:, None, None]
        mag_gap = est_mag - tgt_mag
        log_gap = jnp.log(est_mag) - jnp.log(tgt_mag)
        entries = (usable_count * halfway).astype(jnp.float32)
        spread_list.append(jnp.sum(jnp.where(usable, mag_gap * mag_gap, 0.0), axis=(1, 2)))
        energy_list.append(jnp.sum(jnp.where(usable, tgt_mag * tgt_mag, 0.0), axis=(1, 2)))
        logterm_list.append(
            jnp.sum(jnp.where(usable, log_gap * log_gap, 0.0), axis=(1, 2)) / entries
        )
        saved.append((est_real, est_imag, est_mag, mag_gap, log_gap, usable, entries, table))
    spreads = jnp.stack(spread_list)
    energies = jnp.stack(energy_list)
    logterms = jnp.stack(logterm_list)
    parts = lax.all_gather(jnp.stack([spreads, energies, logterms]), "seg", axis=0, tiled=False)
    spreads, energies, logterms = jnp.sum(parts, axis=0)
    own_loss = jnp.sum(jnp.sqrt((spreads + EPS_RATIO) / energies) + logterms)
    loss = gathered_sum(own_loss, "clip") / (3 * clip_count * lax.axis_size("clip"))
    ratio_weight = 1.0 / jnp.sqrt((spreads + EPS_RATIO) * energies)
    gradient = jnp.zeros((clip_count, samples), jnp.float32)
    extras = []
    for level, points in enumerate(sizes_list):
        stride = points // 4
        frame_count = samples // stride
        est_real, est_imag, est_mag, mag_gap, log_gap, usable, entries, table = saved[level]
        grad_mag = jnp.where(
            usable,
            mag_gap * ratio_weight[level][:, None, None]
            + 2.0 * log_gap / (est_mag * entries[:, None, None]),
            0.0,
        ) * (frames_all * BINS)
        grad_x = jnp.concatenate(
            [grad_mag * est_real / est_mag, grad_mag * est_imag / est_mag], axis=2
        ).astype(jnp.bfloat16)
        grad_frames = jnp.einsum(
            "cfj,jm->cfm", grad_x, table, preferred_element_type=jnp.float32
        )
        spread_back = spread_parts(grad_frames, stride)
        gradient = gradient + spread_back[:, :frame_count].reshape(clip_count, samples)
        extras.append(spread_back[:, frame_count:].reshape(clip_count, 3 * stride))
    halo = 3 * NFFT // 4
    spill = sum(jnp.pad(extra, ((0, 0), (0, halo - extra.shape[1]))) for extra in extras)
    received = shifted(spill, "seg", 1)
    gradient = gradient + jnp.pad(received, ((0, 0), (0, samples - halo)))
    grad_wave = jnp.where(inside, gradient, 0.0).astype(jnp.bfloat16)
    grad_hops = grad_wave.reshape(clip_count, rows_here, HOP)
    portion = lax.all_gather(grad_hops, "seg", axis=1, tiled=True)
    padded = jnp.concatenate([portion, jnp.zeros((clip_count, 3, HOP), portion.dtype)], axis=1)
    grad_signals = jnp.concatenate(
        [padded[:, quarter : quarter + frames_all] for quarter in range(4)], axis=2
    )
    spec_grad = jnp.einsum(
        "ctm,rbm->crbt", grad_signals, local_table, preferred_element_type=jnp.float32
    ).astype(jnp.bfloat16)
    return (loss, spec_grad)


def solution(mesh):
    return jax.shard_map(
        body,
        mesh=mesh,
        in_specs=(P("clip", None, "seg", None), P("clip", "seg"), P("clip")),
        out_specs=(P(), P("clip", None, "seg", None)),
        check_vma=False,
    )
```
